32 devices in a mesh: dp: 4 (over y, x), ctx: 8 (over z, core).
Axes of the slice: x: 2, y: 2, z: 4, core: 2. Of those that a mesh axis runs over, the one named last changes fastest.
Arguments:
- clip_tokens: bfloat16 [4, 2048, 3072], P('dp', 'ctx'), may hold values from -6 to 6
- qkv_weight: bfloat16 [3, 3072, 1536], P(None, None, 'dp'), may hold values from -0.15625 to 0.15625
- out_weight: bfloat16 [1536, 3072], P('dp'), may hold values from -0.5 to 0.5
- neighbours: int32 [32, 10], P('ctx'), may hold values from 0 to 31, as said below
- counts: int32 [32], P('ctx'), may hold values from 2 to 10, as said below
- bias_index: int32 [32, 10], P('ctx'), may hold values from 0 to 342
- rel_bias: float32 [12, 343], P('dp'), may hold values from -4 to 262
Outputs:
- layer_out: bfloat16 [4, 2048, 3072], P('dp', 'ctx')
The draws below stay inside these ranges and needn't reach their ends.
Inputs may be any that keep to these rules, and one draw needn't show every extreme that they name: `neighbours`: tile g lies on ctx index g / 4. Row g starts with g itself; its first counts[g] entries are distinct tiles on ctx indices at most 6 away from that of g; the entries from counts[g] on equal g. Of the tiles of one ctx index, those named in the live entries of the rows of another index are at most 2, and exactly 2 for some pairs of indices. `counts`: some tile has 10 live slots.
All inputs are finite; a program needn't handle non-finite values.
Results may differ from the reference program's by a relative error of at most 0.012.
Values may be sent and summed in bfloat16 or wider, within the bound.
No kernel may reach another device: no remote copies, remote signals or barrier semaphores. Data moves between devices by JAX's collectives and lax.ppermute only.
A program may use at most 128 MiB of HBM per device.

```python
import math
import jax
import jax.numpy as jnp
from jax import lax

D = 3072
HD = 128
HEADS = 12
TILE = 64
REACH = 6
CAP = 2
KMAX = 10
NREL = 343
TPD = 4
TILES = 32
TOKENS = 2048
CLIPS = 4
N_DP = 4
N_CTX = 8


def tile_plan(key):
    base_key = jax.random.fold_in(key, 17)
    key_serve, key_order, key_pick, key_count = jax.random.split(base_key, 4)
    device_ids = jnp.arange(N_CTX, dtype=jnp.int32)
    offsets = jnp.concatenate([jnp.arange(1, REACH + 1, dtype=jnp.int32), -jnp.arange(1, REACH + 1, dtype=jnp.int32)])
    source = device_ids[:, None] - offsets[None, :]
    usable = (source >= 0) & (source < N_CTX)
    served = jax.random.randint(key_serve, (N_CTX, 2 * REACH), 0, CAP + 1)
    served = jnp.where((jnp.abs(offsets) <= 2)[None, :], CAP, served)
    served = jnp.where(usable, served, 0)
    order_score = jax.random.randint(key_order, (N_CTX, 2 * REACH, TPD), 0, 65536) * TPD + jnp.arange(TPD, dtype=jnp.int32)
    ordering = jnp.argsort(order_score, axis=-1, stable=True)[..., :CAP].astype(jnp.int32)
    remote_ids = source[:, :, None] * TPD + ordering
    remote_ok = jnp.arange(CAP)[None, None, :] < served[:, :, None]
    own_ids = device_ids[:, None] * TPD + jnp.arange(TPD, dtype=jnp.int32)[None, :]
    pool_ids = jnp.concatenate([own_ids, remote_ids.reshape(N_CTX, 2 * REACH * CAP)], axis=1)
    pool_ok = jnp.concatenate([jnp.ones((N_CTX, TPD), jnp.bool_), remote_ok.reshape(N_CTX, 2 * REACH * CAP)], axis=1)
    pool_size = TPD + 2 * REACH * CAP
    slots = jnp.arange(pool_size, dtype=jnp.int32)
    tile_slot = jnp.arange(TPD, dtype=jnp.int32)
    random_score = jax.random.randint(key_pick, (N_CTX, TPD, pool_size), 0, 65536) * pool_size + slots[None, None, :]
    own_flag = slots[None, None, :] == tile_slot[None, :, None]
    forced = (slots[None, None, :] >= TPD) & (slots[None, None, :] < TPD + CAP)
    forced = forced & ((slots[None, None, :] - TPD) % TPD == tile_slot[None, :, None]) & pool_ok[:, None, :]
    score = jnp.where(own_flag, 2 ** 29, jnp.where(forced, 2 ** 28, random_score))
    score = jnp.where(pool_ok[:, None, :], score, slots[None, None, :] - pool_size - 1)
    unused_values, chosen = lax.top_k(score, KMAX)
    spread_ids = jnp.broadcast_to(pool_ids[:, None, :], (N_CTX, TPD, pool_size))
    listed = jnp.take_along_axis(spread_ids, chosen, axis=2)
    available = jnp.sum(pool_ok.astype(jnp.int32), axis=1)
    how_many = jax.random.randint(key_count, (N_CTX, TPD), 2, KMAX + 1)
    how_many = jnp.minimum(how_many, available[:, None])
    how_many = how_many.at[0, 0].set(2).at[N_CTX // 2, 0].set(KMAX)
    listed = jnp.where(jnp.arange(KMAX)[None, None, :] < how_many[:, :, None], listed, own_ids[:, :, None])
    return (listed.reshape(TILES, KMAX).astype(jnp.int32), how_many.reshape(TILES).astype(jnp.int32))


def draw_neighbours(key, part):
    return tile_plan(key)[0]


def draw_counts(key, part):
    return tile_plan(key)[1]


def draw_rel_bias(key, part):
    return jnp.clip(jax.random.normal(key, (HEADS, NREL), jnp.float32), -4.0, 4.0)


def place_ends(entries, own_key, least, largest):
    longest = entries.shape.index(max(entries.shape))
    spots = []
    for shift in (0, 1):
        where = [jax.random.randint(jax.random.fold_in(own_key, axis), (), 0, length) for axis, length in enumerate(entries.shape)]
        where[longest] = (where[longest] + shift) % entries.shape[longest]
        spots.append(tuple(where))
    return entries.at[spots[0]].set(least).at[spots[1]].set(largest)


def level_of(own_key, dims, shards, smallest, high):
    def one(axis_at, parts):
        draws = jax.random.uniform(jax.random.fold_in(jax.random.fold_in(own_key, 6), axis_at), (parts,), jnp.float32, smallest / len(shards), high / len(shards))
        return jnp.repeat(jnp.exp(draws), dims[axis_at] // parts).reshape((-1,) + (1,) * (len(dims) - axis_at - 1))

    loudness = one(*shards[0])
    for cut in shards[1:]:
        loudness = loudness * one(*cut)
    return loudness


def gaussian(key, shape, scale, bound, cuts=(), kind=jnp.bfloat16):
    values = jax.random.normal(key, shape, jnp.float32) * scale
    if len(cuts) > 0:
        values = level_of(key, shape, cuts, -0.22, 0.18) * values
    return jnp.clip(values, min=-bound, max=bound).astype(kind)


def setup_inputs(seed: int = 0) -> dict:
    streams_of = jax.random.split(jax.random.key(seed), 8)
    return {
        "clip_tokens": gaussian(streams_of[0], (CLIPS, TOKENS, D), 1.0, 6.0, ((0, 4), (1, 8))),
        "qkv_weight": gaussian(streams_of[1], (3, D, HEADS * HD), (D // 2) ** -0.5, 0.15625, ((2, 4),)),
        "out_weight": gaussian(streams_of[2], (HEADS * HD, D), HD ** -0.5, 0.5, ((0, 4),)),
        "neighbours": draw_neighbours(jax.random.fold_in(streams_of[7], 71), 0),
        "counts": draw_counts(jax.random.fold_in(streams_of[7], 71), 0),
        "bias_index": place_ends(jax.random.randint(streams_of[5], (TILES, KMAX), 0, NREL), jax.random.fold_in(streams_of[5], 1), 0, NREL - 1).astype(jnp.int32),
        "rel_bias": draw_rel_bias(jax.random.fold_in(streams_of[7], 71), 0),
    }


def reference(clip_tokens, qkv_weight, out_weight, neighbours, counts, bias_index, rel_bias):
    clip_count = clip_tokens.shape[0]
    projected = jnp.einsum('ctd,sdh->scth', clip_tokens.astype(jnp.float32), qkv_weight.astype(jnp.float32)).astype(jnp.bfloat16)
    tile_shape = (clip_count, TILES, TILE, HEADS, HD)
    queries = projected[0].reshape(tile_shape)
    key_tiles = projected[1].reshape(tile_shape)
    value_tiles = projected[2].reshape(tile_shape)
    bias_table = rel_bias[:, bias_index]

    def one_block(block_index):
        tile_rows = (block_index * TPD + jnp.arange(TPD)).astype(jnp.int32)
        listed = neighbours[tile_rows]
        near_keys = key_tiles[:, listed].astype(jnp.float32)
        near_values = value_tiles[:, listed].astype(jnp.float32)
        query_tiles = queries[:, tile_rows].astype(jnp.float32)
        scores = jnp.einsum('ctihd,ctmjhd->cthimj', query_tiles, near_keys) * (1.0 / math.sqrt(HD))
        bias_here = jnp.transpose(bias_table[:, tile_rows], (1, 0, 2))
        scores = scores + bias_here[None, :, :, None, :, None]
        live_slots = jnp.arange(KMAX)[None, :] < counts[tile_rows][:, None]
        scores = jnp.where(live_slots[None, :, None, None, :, None], scores, -1e+30)
        row_max = lax.optimization_barrier(jnp.max(scores, axis=(4, 5), keepdims=True))
        weights = jnp.exp(scores - row_max)
        weight_sum = lax.optimization_barrier(jnp.sum(weights, axis=(4, 5)))
        rounded = weights.astype(jnp.bfloat16)
        blended = jnp.einsum('cthimj,ctmjhd->ctihd', rounded.astype(jnp.float32), near_values)
        return (blended / jnp.transpose(weight_sum, (0, 1, 3, 2))[..., None]).astype(jnp.bfloat16)
    blocked = lax.map(one_block, jnp.arange(N_CTX))
    attended = jnp.moveaxis(blocked, 0, 1).reshape(clip_count * TOKENS, HEADS * HD)
    group_width = HEADS // N_DP * HD
    summed = jnp.zeros((clip_count * TOKENS, D), jnp.float32)
    for group_index in range(N_DP):
        low = group_index * group_width
        partial_out = jnp.dot(attended[:, low:low + group_width], out_weight[low:low + group_width], preferred_element_type=jnp.float32).astype(jnp.bfloat16)
        partial_out = lax.optimization_barrier(partial_out)
        summed = summed + partial_out.astype(jnp.float32)
    return summed.astype(jnp.bfloat16).reshape(clip_count, TOKENS, D)
```

```python
import functools
import math

import jax
import jax.numpy as jnp
from jax import lax
from jax.experimental import pallas as pl
from jax.experimental.pallas import tpu as pltpu
from jax.sharding import PartitionSpec as P

TILE = 64
REACH = 6
KMAX = 10
CAP = 2


def shifted(value, axis, steps):
    count = lax.axis_size(axis)
    first, last = (max(0, -steps), min(count, count - steps))
    return lax.ppermute(value, axis, [(source, source + steps) for source in range(first, last)])


def chosen_tiles(rows, rows_live, source, tiles_per_device):
    local = jnp.arange(tiles_per_device, dtype=jnp.int32)
    wanted = source * tiles_per_device + local
    named = jnp.any(
        (rows[:, :, None] == wanted[None, None, :]) & rows_live[:, :, None], axis=(0, 1)
    )
    rank = jnp.cumsum(named.astype(jnp.int32)) - 1
    picks = [
        jnp.sum(jnp.where(named & (rank == slot), local, 0)) for slot in range(CAP)
    ]
    return jnp.stack(picks).astype(jnp.int32)


def attention_kernel(pos_ref, count_ref, bias_ref, q_ref, *refs, heads, head_size, scale):
    kv_refs = refs[:KMAX]
    out_ref = refs[KMAX]
    tile = pl.program_id(0)
    live_count = count_ref[tile]
    queries = q_ref[...]
    clip_count = queries.shape[0]
    for head in range(heads):
        cols = slice(head * head_size, (head + 1) * head_size)
        q_head = queries[:, :, cols]
        scores = []
        for slot in range(KMAX):
            k_head = kv_refs[slot][0, :, :, cols]
            s = lax.dot_general(
                q_head, k_head, (((2,), (2,)), ((0,), (0,))), preferred_element_type=jnp.float32
            )
            s = s * scale + bias_ref[tile, head, slot]
            s = jnp.where(slot < live_count, s, -1e30)
            scores.append(s)
        row_max = scores[0].max(axis=2, keepdims=True)
        for s in scores[1:]:
            row_max = jnp.maximum(row_max, s.max(axis=2, keepdims=True))
        total = jnp.zeros((clip_count, TILE, head_size), jnp.float32)
        weight_sum = jnp.zeros((clip_count, TILE, 1), jnp.float32)
        for slot in range(KMAX):
            w = jnp.exp(scores[slot] - row_max)
            weight_sum = weight_sum + w.sum(axis=2, keepdims=True)
            v_head = kv_refs[slot][1, :, :, cols]
            total = total + lax.dot_general(
                w.astype(jnp.bfloat16), v_head, (((2,), (1,)), ((0,), (0,))),
                preferred_element_type=jnp.float32,
            )
        out_ref[:, :, cols] = (total / weight_sum).astype(out_ref.dtype)


def attend(positions, live_counts, bias, queries, key_values, heads, head_size):
    clip_count, token_count, width = queries.shape
    tile_count = token_count // TILE

    def kv_spec(slot):
        return pl.BlockSpec(
            (None, 2, clip_count, TILE, width),
            lambda t, pos, cnt, slot=slot: (pos[t, slot], 0, 0, 0, 0),
        )

    kernel = functools.partial(
        attention_kernel, heads=heads, head_size=head_size, scale=1.0 / math.sqrt(head_size)
    )
    return pl.pallas_call(
        kernel,
        out_shape=jax.ShapeDtypeStruct(queries.shape, jnp.bfloat16),
        grid_spec=pltpu.PrefetchScalarGridSpec(
            num_scalar_prefetch=2,
            grid=(tile_count,),
            in_specs=[pl.BlockSpec(memory_space=pltpu.SMEM),
                      pl.BlockSpec((clip_count, TILE, width), lambda t, pos, cnt: (0, t, 0))]
            + [kv_spec(slot) for slot in range(KMAX)],
            out_specs=pl.BlockSpec((clip_count, TILE, width), lambda t, pos, cnt: (0, t, 0)),
        ),
    )(positions, live_counts, bias, queries, *([key_values] * KMAX))


def local(clip_tokens, qkv_weight, out_weight, neighbours, counts, bias_index, rel_bias):
    heads_here = rel_bias.shape[0]
    width_here = out_weight.shape[0]
    head_size = width_here // heads_here
    tile_count = clip_tokens.shape[1] // TILE
    n_ctx = lax.axis_size("ctx")
    tokens = lax.all_gather(clip_tokens, "dp", axis=0, tiled=True)
    clip_count = tokens.shape[0]
    projected = jnp.einsum(
        "ctd,sdh->scth", tokens, qkv_weight, preferred_element_type=jnp.float32
    ).astype(jnp.bfloat16)
    queries = projected[0]
    by_tile = projected[1:3].reshape(2, clip_count, tile_count, TILE, width_here)
    by_tile = jnp.transpose(by_tile, (2, 0, 1, 3, 4))
    own_index = lax.axis_index("ctx").astype(jnp.int32)

    all_rows = lax.all_gather(neighbours, "ctx", axis=0, tiled=True)
    all_counts = lax.all_gather(counts, "ctx", axis=0, tiled=True)
    all_live = jnp.arange(KMAX)[None, :] < all_counts[:, None]
    live = jnp.arange(KMAX)[None, :] < counts[:, None]

    offsets = [step for amount in range(1, REACH + 1) for step in (amount, -amount) if amount < n_ctx]
    pieces = [by_tile]
    received_picks = []
    for step in offsets:
        target = own_index + step
        target_rows = lax.dynamic_slice_in_dim(
            all_rows, jnp.clip(target, 0, n_ctx - 1) * tile_count, tile_count, axis=0
        )
        target_live = lax.dynamic_slice_in_dim(
            all_live, jnp.clip(target, 0, n_ctx - 1) * tile_count, tile_count, axis=0
        )
        send_picks = chosen_tiles(target_rows, target_live, own_index, tile_count)
        outgoing = jnp.take(by_tile, send_picks, axis=0)
        pieces.append(shifted(outgoing, "ctx", step))
        received_picks.append(chosen_tiles(neighbours, live, own_index - step, tile_count))
    key_values = jnp.concatenate(pieces, axis=0)

    source = neighbours // tile_count
    within = neighbours % tile_count
    distance = own_index - source
    positions = jnp.where(distance == 0, within, 0)
    for index, step in enumerate(offsets):
        first = received_picks[index][0]
        slot = tile_count + CAP * index + jnp.where(within == first, 0, 1)
        positions = jnp.where(distance == step, slot, positions)
    positions = positions.astype(jnp.int32)

    bias = jnp.transpose(jnp.take(rel_bias, bias_index, axis=1), (1, 0, 2))
    attended = attend(positions, counts.astype(jnp.int32), bias, queries, key_values, heads_here, head_size)
    partial_out = jnp.einsum(
        "cth,hd->ctd", attended, out_weight, preferred_element_type=jnp.float32
    ).astype(jnp.bfloat16)
    return lax.psum_scatter(partial_out, "dp", scatter_dimension=0, tiled=True)


def solution(mesh):
    placed = (
        P("dp", "ctx", None),
        P(None, None, "dp"),
        P("dp", None),
        P("ctx", None),
        P("ctx"),
        P("ctx", None),
        P("dp", None),
    )
    return jax.shard_map(
        local, mesh=mesh, in_specs=placed, out_specs=P("dp", "ctx", None), check_vma=False
    )
```

```python
import functools
import math

import jax
import jax.numpy as jnp
from jax import lax
from jax.experimental import pallas as pl
from jax.experimental.pallas import tpu as pltpu
from jax.sharding import PartitionSpec as P

TILE = 64
REACH = 6
KMAX = 10
CAP = 2


def shifted(value, axis, steps):
    count = lax.axis_size(axis)
    first, last = (max(0, -steps), min(count, count - steps))
    return lax.ppermute(value, axis, [(source, source + steps) for source in range(first, last)])


def chosen_tiles(rows, rows_live, source, tiles_per_device):
    local = jnp.arange(tiles_per_device, dtype=jnp.int32)
    wanted = source * tiles_per_device + local
    named = jnp.any(
        (rows[:, :, None] == wanted[None, None, :]) & rows_live[:, :, None], axis=(0, 1)
    )
    rank = jnp.cumsum(named.astype(jnp.int32)) - 1
    picks = [
        jnp.sum(jnp.where(named & (rank == slot), local, 0)) for slot in range(CAP)
    ]
    return jnp.stack(picks).astype(jnp.int32)


def attention_kernel(pos_ref, count_ref, bias_ref, q_ref, *refs, heads, head_size, scale):
    kv_refs = refs[:KMAX]
    out_ref = refs[KMAX]
    tile = pl.program_id(0)
    live_count = count_ref[tile]
    queries = q_ref[...]
    clip_count = queries.shape[0]
    for head in range(heads):
        cols = slice(head * head_size, (head + 1) * head_size)
        q_head = queries[:, :, cols]
        scores = []
        for slot in range(KMAX):
            k_head = kv_refs[slot][0, :, :, cols]
            s = lax.dot_general(
                q_head, k_head, (((2,), (2,)), ((0,), (0,))), preferred_element_type=jnp.float32
            )
            s = s * scale + bias_ref[tile, head, slot]
            s = jnp.where(slot < live_count, s, -1e30)
            scores.append(s)
        row_max = scores[0].max(axis=2, keepdims=True)
        for s in scores[1:]:
            row_max = jnp.maximum(row_max, s.max(axis=2, keepdims=True))
        total = jnp.zeros((clip_count, TILE, head_size), jnp.float32)
        weight_sum = jnp.zeros((clip_count, TILE, 1), jnp.float32)
        for slot in range(KMAX):
            w = jnp.exp(scores[slot] - row_max)
            weight_sum = weight_sum + w.sum(axis=2, keepdims=True)
            v_head = kv_refs[slot][1, :, :, cols]
            total = total + lax.dot_general(
                w.astype(jnp.bfloat16), v_head, (((2,), (1,)), ((0,), (0,))),
                preferred_element_type=jnp.float32,
            )
        out_ref[:, :, cols] = (total / weight_sum).astype(out_ref.dtype)


def attend(positions, live_counts, bias, queries, key_values, heads, head_size):
    clip_count, token_count, width = queries.shape
    tile_count = token_count // TILE

    def kv_spec(slot):
        return pl.BlockSpec(
            (None, 2, clip_count, TILE, width),
            lambda t, pos, cnt, slot=slot: (pos[t, slot], 0, 0, 0, 0),
        )

    kernel = functools.partial(
        attention_kernel, heads=heads, head_size=head_size, scale=1.0 / math.sqrt(head_size)
    )
    return pl.pallas_call(
        kernel,
        out_shape=jax.ShapeDtypeStruct(queries.shape, jnp.bfloat16),
        grid_spec=pltpu.PrefetchScalarGridSpec(
            num_scalar_prefetch=2,
            grid=(tile_count,),
            in_specs=[pl.BlockSpec(memory_space=pltpu.SMEM),
                      pl.BlockSpec((clip_count, TILE, width), lambda t, pos, cnt: (0, t, 0))]
            + [kv_spec(slot) for slot in range(KMAX)],
            out_specs=pl.BlockSpec((clip_count, TILE, width), lambda t, pos, cnt: (0, t, 0)),
        ),
    )(positions, live_counts, bias, queries, *([key_values] * KMAX))


def partner_pairs(count, step):
    return [(source, source ^ step) for source in range(count)]


def local(clip_tokens, qkv_weight, out_weight, neighbours, counts, bias_index, rel_bias):
    heads_here = rel_bias.shape[0]
    width_here = out_weight.shape[0]
    head_size = width_here // heads_here
    token_count = clip_tokens.shape[1]
    tile_count = token_count // TILE
    n_ctx = lax.axis_size("ctx")
    n_dp = lax.axis_size("dp")
    own_index = lax.axis_index("ctx").astype(jnp.int32)

    table = jnp.concatenate([neighbours, counts[:, None]], axis=1)
    all_table = lax.all_gather(table, "ctx", axis=0, tiled=True)
    all_rows = all_table[:, :KMAX]
    all_live = jnp.arange(KMAX)[None, :] < all_table[:, KMAX:]
    live = jnp.arange(KMAX)[None, :] < counts[:, None]

    offsets = [step for amount in range(1, REACH + 1) for step in (amount, -amount) if amount < n_ctx]
    send_picks = []
    received_picks = []
    for step in offsets:
        target = jnp.clip(own_index + step, 0, n_ctx - 1) * tile_count
        target_rows = lax.dynamic_slice_in_dim(all_rows, target, tile_count, axis=0)
        target_live = lax.dynamic_slice_in_dim(all_live, target, tile_count, axis=0)
        send_picks.append(chosen_tiles(target_rows, target_live, own_index, tile_count))
        received_picks.append(chosen_tiles(neighbours, live, own_index - step, tile_count))

    source = neighbours // tile_count
    within = neighbours % tile_count
    distance = own_index - source
    positions = jnp.where(distance == 0, within, 0)
    for index, step in enumerate(offsets):
        first = received_picks[index][0]
        slot = tile_count + CAP * index + jnp.where(within == first, 0, 1)
        positions = jnp.where(distance == step, slot, positions)
    positions = positions.astype(jnp.int32)
    bias = jnp.transpose(jnp.take(rel_bias, bias_index, axis=1), (1, 0, 2))
    live_counts = counts.astype(jnp.int32)

    own_tokens = clip_tokens[0]
    clip_inputs = [own_tokens] + [
        lax.ppermute(own_tokens, "dp", partner_pairs(n_dp, step)) for step in range(1, n_dp)
    ]
    total = None
    for step in range(n_dp):
        projected = jnp.einsum(
            "td,sdh->sth", clip_inputs[step], qkv_weight, preferred_element_type=jnp.float32
        ).astype(jnp.bfloat16)
        queries = projected[0][None]
        by_tile = jnp.transpose(
            projected[1:3].reshape(2, tile_count, TILE, width_here), (1, 0, 2, 3)
        )[:, :, None]
        pieces = [by_tile]
        for index, offset in enumerate(offsets):
            outgoing = jnp.take(by_tile, send_picks[index], axis=0)
            pieces.append(shifted(outgoing, "ctx", offset))
        key_values = jnp.concatenate(pieces, axis=0)
        attended = attend(positions, live_counts, bias, queries, key_values, heads_here, head_size)
        partial_out = jnp.dot(
            attended[0], out_weight, preferred_element_type=jnp.float32
        ).astype(jnp.bfloat16)
        if step > 0:
            partial_out = lax.ppermute(partial_out, "dp", partner_pairs(n_dp, step))
        contribution = partial_out.astype(jnp.float32)
        total = contribution if total is None else total + contribution
    return total.astype(jnp.bfloat16)[None]


def solution(mesh):
    placed = (
        P("dp", "ctx", None),
        P(None, None, "dp"),
        P("dp", None),
        P("ctx", None),
        P("ctx"),
        P("ctx", None),
        P("dp", None),
    )
    return jax.shard_map(
        local, mesh=mesh, in_specs=placed, out_specs=P("dp", "ctx", None), check_vma=False
    )
```

```python
import functools
import math

import jax
import jax.numpy as jnp
from jax import lax
from jax.experimental import pallas as pl
from jax.experimental.pallas import tpu as pltpu
from jax.sharding import PartitionSpec as P

TILE = 64
REACH = 6
KMAX = 10
CAP = 2


def first_two(rows, rows_live, sources, tiles_per_device):
    local = jnp.arange(tiles_per_device, dtype=jnp.int32)
    wanted = sources[:, None] * tiles_per_device + local[None, :]
    named = jnp.any(
        (rows[:, :, :, None] == wanted[:, None, None, :]) & rows_live[:, :, :, None], axis=(1, 2)
    )
    order = jnp.where(named, local[None, :], tiles_per_device)
    first = jnp.min(order, axis=1)
    second = jnp.min(jnp.where(order > first[:, None], order, tiles_per_device), axis=1)
    first = jnp.where(first == tiles_per_device, 0, first)
    second = jnp.where(second == tiles_per_device, 0, second)
    return first.astype(jnp.int32), second.astype(jnp.int32)


def attention_kernel(pos_ref, count_ref, bias_ref, q_ref, *refs, heads, head_size, scale):
    kv_refs = refs[:KMAX]
    out_ref = refs[KMAX]
    tile = pl.program_id(0)
    live_count = count_ref[tile]
    queries = q_ref[...]
    clip_count = queries.shape[0]
    for head in range(heads):
        cols = slice(head * head_size, (head + 1) * head_size)
        q_head = queries[:, :, cols]
        scores = []
        for slot in range(KMAX):
            k_head = kv_refs[slot][0, :, :, cols]
            s = lax.dot_general(
                q_head, k_head, (((2,), (2,)), ((0,), (0,))), preferred_element_type=jnp.float32
            )
            s = s * scale + bias_ref[tile, head, slot]
            s = jnp.where(slot < live_count, s, -1e30)
            scores.append(s)
        row_max = scores[0].max(axis=2, keepdims=True)
        for s in scores[1:]:
            row_max = jnp.maximum(row_max, s.max(axis=2, keepdims=True))
        total = jnp.zeros((clip_count, TILE, head_size), jnp.float32)
        weight_sum = jnp.zeros((clip_count, TILE, 1), jnp.float32)
        for slot in range(KMAX):
            w = jnp.exp(scores[slot] - row_max)
            weight_sum = weight_sum + w.sum(axis=2, keepdims=True)
            v_head = kv_refs[slot][1, :, :, cols]
            total = total + lax.dot_general(
                w.astype(jnp.bfloat16), v_head, (((2,), (1,)), ((0,), (0,))),
                preferred_element_type=jnp.float32,
            )
        out_ref[:, :, cols] = (total / weight_sum).astype(out_ref.dtype)


def attend(positions, live_counts, bias, queries, key_values, heads, head_size):
    clip_count, token_count, width = queries.shape
    tile_count = token_count // TILE

    def kv_spec(slot):
        return pl.BlockSpec(
            (None, 2, clip_count, TILE, width),
            lambda t, pos, cnt, slot=slot: (pos[t, slot], 0, 0, 0, 0),
        )

    kernel = functools.partial(
        attention_kernel, heads=heads, head_size=head_size, scale=1.0 / math.sqrt(head_size)
    )
    return pl.pallas_call(
        kernel,
        out_shape=jax.ShapeDtypeStruct(queries.shape, jnp.bfloat16),
        grid_spec=pltpu.PrefetchScalarGridSpec(
            num_scalar_prefetch=2,
            grid=(tile_count,),
            in_specs=[pl.BlockSpec(memory_space=pltpu.SMEM),
                      pl.BlockSpec((clip_count, TILE, width), lambda t, pos, cnt: (0, t, 0))]
            + [kv_spec(slot) for slot in range(KMAX)],
            out_specs=pl.BlockSpec((clip_count, TILE, width), lambda t, pos, cnt: (0, t, 0)),
        ),
    )(positions, live_counts, bias, queries, *([key_values] * KMAX))


def partner_pairs(count, step):
    return [(source, source ^ step) for source in range(count)]


def local(clip_tokens, qkv_weight, out_weight, neighbours, counts, bias_index, rel_bias):
    heads_here = rel_bias.shape[0]
    width_here = out_weight.shape[0]
    head_size = width_here // heads_here
    token_count = clip_tokens.shape[1]
    tile_count = token_count // TILE
    n_ctx = lax.axis_size("ctx")
    n_dp = lax.axis_size("dp")
    own_index = lax.axis_index("ctx").astype(jnp.int32)
    devices = jnp.arange(n_ctx, dtype=jnp.int32)

    table = jnp.concatenate([neighbours, counts[:, None]], axis=1).astype(jnp.float32)
    all_table = lax.all_gather(table, "ctx", axis=0, tiled=True).astype(jnp.int32)
    all_table = all_table.reshape(n_ctx, tile_count, KMAX + 1)
    all_live = jnp.arange(KMAX)[None, None, :] < all_table[:, :, KMAX:]
    send_first, send_second = first_two(
        all_table[:, :, :KMAX], all_live, jnp.full((n_ctx,), own_index), tile_count
    )
    send_picks = jnp.stack([send_first, send_second], axis=1).reshape(-1)

    live = jnp.arange(KMAX)[None, :] < counts[:, None]
    recv_first, _ = first_two(
        jnp.broadcast_to(neighbours[None], (n_ctx,) + neighbours.shape),
        jnp.broadcast_to(live[None], (n_ctx,) + live.shape),
        devices,
        tile_count,
    )
    source = neighbours // tile_count
    within = neighbours % tile_count
    remote_slot = tile_count + CAP * source + jnp.where(within == recv_first[source], 0, 1)
    positions = jnp.where(source == own_index, within, remote_slot).astype(jnp.int32)
    bias = jnp.transpose(jnp.take(rel_bias, bias_index, axis=1), (1, 0, 2))
    live_counts = counts.astype(jnp.int32)

    own_tokens = clip_tokens[0]
    clip_inputs = [own_tokens] + [
        lax.ppermute(own_tokens, "dp", partner_pairs(n_dp, step)) for step in range(1, n_dp)
    ]
    total = None
    for step in range(n_dp):
        projected = jnp.einsum(
            "td,sdh->sth", clip_inputs[step], qkv_weight, preferred_element_type=jnp.float32
        ).astype(jnp.bfloat16)
        queries = projected[0][None]
        by_tile = jnp.transpose(
            projected[1:3].reshape(2, tile_count, TILE, width_here), (1, 0, 2, 3)
        )[:, :, None]
        outgoing = jnp.take(by_tile, send_picks, axis=0)
        incoming = lax.all_to_all(outgoing, "ctx", 0, 0, tiled=True)
        key_values = jnp.concatenate([by_tile, incoming], axis=0)
        attended = attend(positions, live_counts, bias, queries, key_values, heads_here, head_size)
        partial_out = jnp.dot(
            attended[0], out_weight, preferred_element_type=jnp.float32
        ).astype(jnp.bfloat16)
        if step > 0:
            partial_out = lax.ppermute(partial_out, "dp", partner_pairs(n_dp, step))
        contribution = partial_out.astype(jnp.float32)
        total = contribution if total is None else total + contribution
    return total.astype(jnp.bfloat16)[None]


def solution(mesh):
    placed = (
        P("dp", "ctx", None),
        P(None, None, "dp"),
        P("dp", None),
        P("ctx", None),
        P("ctx"),
        P("ctx", None),
        P("dp", None),
    )
    return jax.shard_map(
        local, mesh=mesh, in_specs=placed, out_specs=P("dp", "ctx", None), check_vma=False
    )
```

```python
import functools
import math

import jax
import jax.numpy as jnp
from jax import lax
from jax.experimental import pallas as pl
from jax.experimental.pallas import tpu as pltpu
from jax.sharding import PartitionSpec as P

TILE = 64
REACH = 6
KMAX = 10
CAP = 2


def first_two(rows, rows_live, sources, tiles_per_device):
    local = jnp.arange(tiles_per_device, dtype=jnp.int32)
    wanted = sources[:, None] * tiles_per_device + local[None, :]
    named = jnp.any(
        (rows[:, :, :, None] == wanted[:, None, None, :]) & rows_live[:, :, :, None], axis=(1, 2)
    )
    order = jnp.where(named, local[None, :], tiles_per_device)
    first = jnp.min(order, axis=1)
    second = jnp.min(jnp.where(order > first[:, None], order, tiles_per_device), axis=1)
    first = jnp.where(first == tiles_per_device, 0, first)
    second = jnp.where(second == tiles_per_device, 0, second)
    return first.astype(jnp.int32), second.astype(jnp.int32)


def attention_kernel(pos_ref, count_ref, bias_ref, q_ref, *refs, heads, head_size, scale):
    kv_refs = refs[:KMAX]
    out_ref = refs[KMAX]
    tile = pl.program_id(0)
    live_count = count_ref[tile]
    queries = q_ref[...]
    clip_count = queries.shape[0]
    for head in range(heads):
        cols = slice(head * head_size, (head + 1) * head_size)
        q_head = queries[:, :, cols]
        scores = []
        for slot in range(KMAX):
            k_head = kv_refs[slot][0, :, :, cols]
            s = lax.dot_general(
                q_head, k_head, (((2,), (2,)), ((0,), (0,))), preferred_element_type=jnp.float32
            )
            s = s * scale + bias_ref[tile, head, slot]
            s = jnp.where(slot < live_count, s, -1e30)
            scores.append(s)
        row_max = scores[0].max(axis=2, keepdims=True)
        for s in scores[1:]:
            row_max = jnp.maximum(row_max, s.max(axis=2, keepdims=True))
        total = jnp.zeros((clip_count, TILE, head_size), jnp.float32)
        weight_sum = jnp.zeros((clip_count, TILE, 1), jnp.float32)
        for slot in range(KMAX):
            w = jnp.exp(scores[slot] - row_max)
            weight_sum = weight_sum + w.sum(axis=2, keepdims=True)
            v_head = kv_refs[slot][1, :, :, cols]
            total = total + lax.dot_general(
                w.astype(jnp.bfloat16), v_head, (((2,), (1,)), ((0,), (0,))),
                preferred_element_type=jnp.float32,
            )
        out_ref[:, :, cols] = (total / weight_sum).astype(out_ref.dtype)


def attend(positions, live_counts, bias, queries, key_values, heads, head_size):
    clip_count, token_count, width = queries.shape
    tile_count = token_count // TILE

    def kv_spec(slot):
        return pl.BlockSpec(
            (None, 2, clip_count, TILE, width),
            lambda t, pos, cnt, slot=slot: (pos[t, slot], 0, 0, 0, 0),
        )

    kernel = functools.partial(
        attention_kernel, heads=heads, head_size=head_size, scale=1.0 / math.sqrt(head_size)
    )
    return pl.pallas_call(
        kernel,
        out_shape=jax.ShapeDtypeStruct(queries.shape, jnp.bfloat16),
        grid_spec=pltpu.PrefetchScalarGridSpec(
            num_scalar_prefetch=2,
            grid=(tile_count,),
            in_specs=[pl.BlockSpec(memory_space=pltpu.SMEM),
                      pl.BlockSpec((clip_count, TILE, width), lambda t, pos, cnt: (0, t, 0))]
            + [kv_spec(slot) for slot in range(KMAX)],
            out_specs=pl.BlockSpec((clip_count, TILE, width), lambda t, pos, cnt: (0, t, 0)),
        ),
    )(positions, live_counts, bias, queries, *([key_values] * KMAX))


def partner_pairs(count, step):
    return [(source, source ^ step) for source in range(count)]


def local(clip_tokens, qkv_weight, out_weight, neighbours, counts, bias_index, rel_bias):
    heads_here = rel_bias.shape[0]
    width_here = out_weight.shape[0]
    head_size = width_here // heads_here
    token_count = clip_tokens.shape[1]
    tile_count = token_count // TILE
    n_ctx = lax.axis_size("ctx")
    n_dp = lax.axis_size("dp")
    own_index = lax.axis_index("ctx").astype(jnp.int32)
    devices = jnp.arange(n_ctx, dtype=jnp.int32)

    table = jnp.concatenate([neighbours, counts[:, None]], axis=1).astype(jnp.float32)
    all_table = lax.all_gather(table, "ctx", axis=0, tiled=True).astype(jnp.int32)
    all_table = all_table.reshape(n_ctx, tile_count, KMAX + 1)
    all_live = jnp.arange(KMAX)[None, None, :] < all_table[:, :, KMAX:]
    send_first, send_second = first_two(
        all_table[:, :, :KMAX], all_live, jnp.full((n_ctx,), own_index), tile_count
    )
    send_picks = jnp.stack([send_first, send_second], axis=1).reshape(-1)

    live = jnp.arange(KMAX)[None, :] < counts[:, None]
    recv_first, _ = first_two(
        jnp.broadcast_to(neighbours[None], (n_ctx,) + neighbours.shape),
        jnp.broadcast_to(live[None], (n_ctx,) + live.shape),
        devices,
        tile_count,
    )
    source = neighbours // tile_count
    within = neighbours % tile_count
    remote_slot = tile_count + CAP * source + jnp.where(within == recv_first[source], 0, 1)
    positions = jnp.where(source == own_index, within, remote_slot).astype(jnp.int32)
    bias = jnp.transpose(jnp.take(rel_bias, bias_index, axis=1), (1, 0, 2))
    live_counts = counts.astype(jnp.int32)

    own_tokens = clip_tokens[0]
    order = list(range(1, n_dp)) + [0]
    clip_inputs = {0: own_tokens}
    for step in range(1, n_dp):
        clip_inputs[step] = lax.ppermute(own_tokens, "dp", partner_pairs(n_dp, step))
    outgoing = {}
    for step in order:
        projected = jnp.einsum(
            "td,sdh->sth", clip_inputs[step], qkv_weight, preferred_element_type=jnp.float32
        ).astype(jnp.bfloat16)
        by_tile = jnp.transpose(
            projected[1:3].reshape(2, tile_count, TILE, width_here), (1, 0, 2, 3)
        )[:, :, None]
        outgoing[step] = (projected[0][None], by_tile, jnp.take(by_tile, send_picks, axis=0))
    total = None
    finished = []
    for index, step in enumerate(order):
        queries, by_tile, payload = outgoing[step]
        if index >= 2:
            payload, _ = lax.optimization_barrier((payload, finished[index - 2]))
        incoming = lax.all_to_all(payload, "ctx", 0, 0, tiled=True)
        key_values = jnp.concatenate([by_tile, incoming], axis=0)
        attended = attend(positions, live_counts, bias, queries, key_values, heads_here, head_size)
        finished.append(attended)
        partial_out = jnp.dot(
            attended[0], out_weight, preferred_element_type=jnp.float32
        ).astype(jnp.bfloat16)
        if step > 0:
            partial_out = lax.ppermute(partial_out, "dp", partner_pairs(n_dp, step))
        contribution = partial_out.astype(jnp.float32)
        total = contribution if total is None else total + contribution
    return total.astype(jnp.bfloat16)[None]


def solution(mesh):
    placed = (
        P("dp", "ctx", None),
        P(None, None, "dp"),
        P("dp", None),
        P("ctx", None),
        P("ctx"),
        P("ctx", None),
        P("dp", None),
    )
    return jax.shard_map(
        local, mesh=mesh, in_specs=placed, out_specs=P("dp", "ctx", None), check_vma=False
    )
```

```python
import functools
import math

import jax
import jax.numpy as jnp
from jax import lax
from jax.experimental import pallas as pl
from jax.experimental.pallas import tpu as pltpu
from jax.sharding import PartitionSpec as P

TILE = 64
REACH = 6
KMAX = 10
CAP = 2


def first_two(rows, rows_live, sources, tiles_per_device):
    local = jnp.arange(tiles_per_device, dtype=jnp.int32)
    wanted = sources[:, None] * tiles_per_device + local[None, :]
    named = jnp.any(
        (rows[:, :, :, None] == wanted[:, None, None, :]) & rows_live[:, :, :, None], axis=(1, 2)
    )
    order = jnp.where(named, local[None, :], tiles_per_device)
    first = jnp.min(order, axis=1)
    second = jnp.min(jnp.where(order > first[:, None], order, tiles_per_device), axis=1)
    first = jnp.where(first == tiles_per_device, 0, first)
    second = jnp.where(second == tiles_per_device, 0, second)
    return first.astype(jnp.int32), second.astype(jnp.int32)


def attention_kernel(pos_ref, count_ref, bias_ref, q_ref, *refs, heads, head_size, scale):
    kv_refs = refs[:KMAX]
    out_ref = refs[KMAX]
    tile = pl.program_id(0)
    live_count = count_ref[tile]
    queries = q_ref[...]
    clip_count = queries.shape[0]
    for head in range(heads):
        cols = slice(head * head_size, (head + 1) * head_size)
        q_head = queries[:, :, cols]
        scores = []
        for slot in range(KMAX):
            k_head = kv_refs[slot][0, :, :, cols]
            s = lax.dot_general(
                q_head, k_head, (((2,), (2,)), ((0,), (0,))), preferred_element_type=jnp.float32
            )
            s = s * scale + bias_ref[tile, head, slot]
            s = jnp.where(slot < live_count, s, -1e30)
            scores.append(s)
        row_max = scores[0].max(axis=2, keepdims=True)
        for s in scores[1:]:
            row_max = jnp.maximum(row_max, s.max(axis=2, keepdims=True))
        total = jnp.zeros((clip_count, TILE, head_size), jnp.float32)
        weight_sum = jnp.zeros((clip_count, TILE, 1), jnp.float32)
        for slot in range(KMAX):
            w = jnp.exp(scores[slot] - row_max)
            weight_sum = weight_sum + w.sum(axis=2, keepdims=True)
            v_head = kv_refs[slot][1, :, :, cols]
            total = total + lax.dot_general(
                w.astype(jnp.bfloat16), v_head, (((2,), (1,)), ((0,), (0,))),
                preferred_element_type=jnp.float32,
            )
        out_ref[:, :, cols] = (total / weight_sum).astype(out_ref.dtype)


def attend(positions, live_counts, bias, queries, key_values, heads, head_size):
    clip_count, token_count, width = queries.shape
    tile_count = token_count // TILE

    def kv_spec(slot):
        return pl.BlockSpec(
            (None, 2, clip_count, TILE, width),
            lambda t, pos, cnt, slot=slot: (pos[t, slot], 0, 0, 0, 0),
        )

    kernel = functools.partial(
        attention_kernel, heads=heads, head_size=head_size, scale=1.0 / math.sqrt(head_size)
    )
    return pl.pallas_call(
        kernel,
        out_shape=jax.ShapeDtypeStruct(queries.shape, jnp.bfloat16),
        grid_spec=pltpu.PrefetchScalarGridSpec(
            num_scalar_prefetch=2,
            grid=(tile_count,),
            in_specs=[pl.BlockSpec(memory_space=pltpu.SMEM),
                      pl.BlockSpec((clip_count, TILE, width), lambda t, pos, cnt: (0, t, 0))]
            + [kv_spec(slot) for slot in range(KMAX)],
            out_specs=pl.BlockSpec((clip_count, TILE, width), lambda t, pos, cnt: (0, t, 0)),
        ),
    )(positions, live_counts, bias, queries, *([key_values] * KMAX))


def partner_pairs(count, step):
    return [(source, source ^ step) for source in range(count)]


def local(clip_tokens, qkv_weight, out_weight, neighbours, counts, bias_index, rel_bias):
    heads_here = rel_bias.shape[0]
    width_here = out_weight.shape[0]
    head_size = width_here // heads_here
    token_count = clip_tokens.shape[1]
    tile_count = token_count // TILE
    n_ctx = lax.axis_size("ctx")
    n_dp = lax.axis_size("dp")
    own_index = lax.axis_index("ctx").astype(jnp.int32)
    devices = jnp.arange(n_ctx, dtype=jnp.int32)

    table = jnp.concatenate([neighbours, counts[:, None]], axis=1).astype(jnp.float32)
    all_table = lax.all_gather(table, "ctx", axis=0, tiled=True).astype(jnp.int32)
    all_table = all_table.reshape(n_ctx, tile_count, KMAX + 1)
    all_live = jnp.arange(KMAX)[None, None, :] < all_table[:, :, KMAX:]
    send_first, send_second = first_two(
        all_table[:, :, :KMAX], all_live, jnp.full((n_ctx,), own_index), tile_count
    )
    send_picks = jnp.stack([send_first, send_second], axis=1).reshape(-1)

    live = jnp.arange(KMAX)[None, :] < counts[:, None]
    recv_first, _ = first_two(
        jnp.broadcast_to(neighbours[None], (n_ctx,) + neighbours.shape),
        jnp.broadcast_to(live[None], (n_ctx,) + live.shape),
        devices,
        tile_count,
    )
    source = neighbours // tile_count
    within = neighbours % tile_count
    remote_slot = tile_count + CAP * source + jnp.where(within == recv_first[source], 0, 1)
    positions = jnp.where(source == own_index, within, remote_slot).astype(jnp.int32)
    bias = jnp.transpose(jnp.take(rel_bias, bias_index, axis=1), (1, 0, 2))
    live_counts = counts.astype(jnp.int32)

    own_tokens = clip_tokens[0]
    order = [1, 3, 2, 0] if n_dp == 4 else list(range(1, n_dp)) + [0]
    arrived = {0: own_tokens}
    for step in range(1, n_dp):
        arrived[step] = lax.ppermute(own_tokens, "dp", partner_pairs(n_dp, step))
    total = None
    received = []
    partials = []
    for index, step in enumerate(order):
        tokens = arrived[step]
        if index >= 1:
            tokens, _ = lax.optimization_barrier((tokens, received[max(index - 2, 0)]))
        projected = jnp.einsum(
            "td,sdh->sth", tokens, qkv_weight, preferred_element_type=jnp.float32
        ).astype(jnp.bfloat16)
        queries = projected[0][None]
        by_tile = jnp.transpose(
            projected[1:3].reshape(2, tile_count, TILE, width_here), (1, 0, 2, 3)
        )[:, :, None]
        payload = jnp.take(by_tile, send_picks, axis=0)
        if index >= 2:
            payload, _ = lax.optimization_barrier((payload, partials[index - 2]))
        incoming = lax.all_to_all(payload, "ctx", 0, 0, tiled=True)
        received.append(incoming)
        key_values = jnp.concatenate([by_tile, incoming], axis=0)
        attended = attend(positions, live_counts, bias, queries, key_values, heads_here, head_size)
        partial_out = jnp.dot(
            attended[0], out_weight, preferred_element_type=jnp.float32
        ).astype(jnp.bfloat16)
        partials.append(partial_out)
        if step > 0:
            partial_out = lax.ppermute(partial_out, "dp", partner_pairs(n_dp, step))
        contribution = partial_out.astype(jnp.float32)
        total = contribution if total is None else total + contribution
    return total.astype(jnp.bfloat16)[None]


def solution(mesh):
    placed = (
        P("dp", "ctx", None),
        P(None, None, "dp"),
        P("dp", None),
        P("ctx", None),
        P("ctx"),
        P("ctx", None),
        P("dp", None),
    )
    return jax.shard_map(
        local, mesh=mesh, in_specs=placed, out_specs=P("dp", "ctx", None), check_vma=False
    )
```

```python
import functools
import math

import jax
import jax.numpy as jnp
from jax import lax
from jax.experimental import pallas as pl
from jax.experimental.pallas import tpu as pltpu
from jax.sharding import PartitionSpec as P

TILE = 64
REACH = 6
KMAX = 10
CAP = 2


def first_two(rows, rows_live, sources, tiles_per_device):
    local = jnp.arange(tiles_per_device, dtype=jnp.int32)
    wanted = sources[:, None] * tiles_per_device + local[None, :]
    named = jnp.any(
        (rows[:, :, :, None] == wanted[:, None, None, :]) & rows_live[:, :, :, None], axis=(1, 2)
    )
    order = jnp.where(named, local[None, :], tiles_per_device)
    first = jnp.min(order, axis=1)
    second = jnp.min(jnp.where(order > first[:, None], order, tiles_per_device), axis=1)
    first = jnp.where(first == tiles_per_device, 0, first)
    second = jnp.where(second == tiles_per_device, 0, second)
    return first.astype(jnp.int32), second.astype(jnp.int32)


def attention_kernel(pos_ref, count_ref, bias_ref, q_ref, *refs, heads, head_size, scale):
    kv_refs = refs[:KMAX]
    out_ref = refs[KMAX]
    tile = pl.program_id(0)
    live_count = count_ref[tile]
    queries = q_ref[...]
    clip_count = queries.shape[0]
    for head in range(heads):
        cols = slice(head * head_size, (head + 1) * head_size)
        q_head = queries[:, :, cols]
        scores = []
        for slot in range(KMAX):
            k_head = kv_refs[slot][0, :, :, cols]
            s = lax.dot_general(
                q_head, k_head, (((2,), (2,)), ((0,), (0,))), preferred_element_type=jnp.float32
            )
            s = s * scale + bias_ref[tile, head, slot]
            s = jnp.where(slot < live_count, s, -1e30)
            scores.append(s)
        row_max = scores[0].max(axis=2, keepdims=True)
        for s in scores[1:]:
            row_max = jnp.maximum(row_max, s.max(axis=2, keepdims=True))
        total = jnp.zeros((clip_count, TILE, head_size), jnp.float32)
        weight_sum = jnp.zeros((clip_count, TILE, 1), jnp.float32)
        for slot in range(KMAX):
            w = jnp.exp(scores[slot] - row_max)
            weight_sum = weight_sum + w.sum(axis=2, keepdims=True)
            v_head = kv_refs[slot][1, :, :, cols]
            total = total + lax.dot_general(
                w.astype(jnp.bfloat16), v_head, (((2,), (1,)), ((0,), (0,))),
                preferred_element_type=jnp.float32,
            )
        out_ref[:, :, cols] = (total / weight_sum).astype(out_ref.dtype)


def attend(positions, live_counts, bias, queries, key_values, heads, head_size):
    clip_count, token_count, width = queries.shape
    tile_count = token_count // TILE

    def kv_spec(slot):
        return pl.BlockSpec(
            (None, 2, clip_count, TILE, width),
            lambda t, pos, cnt, slot=slot: (pos[t, slot], 0, 0, 0, 0),
        )

    kernel = functools.partial(
        attention_kernel, heads=heads, head_size=head_size, scale=1.0 / math.sqrt(head_size)
    )
    return pl.pallas_call(
        kernel,
        out_shape=jax.ShapeDtypeStruct(queries.shape, jnp.bfloat16),
        grid_spec=pltpu.PrefetchScalarGridSpec(
            num_scalar_prefetch=2,
            grid=(tile_count,),
            in_specs=[pl.BlockSpec(memory_space=pltpu.SMEM),
                      pl.BlockSpec((clip_count, TILE, width), lambda t, pos, cnt: (0, t, 0))]
            + [kv_spec(slot) for slot in range(KMAX)],
            out_specs=pl.BlockSpec((clip_count, TILE, width), lambda t, pos, cnt: (0, t, 0)),
        ),
    )(positions, live_counts, bias, queries, *([key_values] * KMAX))


def partner_pairs(count, step):
    return [(source, source ^ step) for source in range(count)]


def local(clip_tokens, qkv_weight, out_weight, neighbours, counts, bias_index, rel_bias):
    heads_here = rel_bias.shape[0]
    width_here = out_weight.shape[0]
    head_size = width_here // heads_here
    token_count = clip_tokens.shape[1]
    tile_count = token_count // TILE
    n_ctx = lax.axis_size("ctx")
    n_dp = lax.axis_size("dp")
    own_index = lax.axis_index("ctx").astype(jnp.int32)
    devices = jnp.arange(n_ctx, dtype=jnp.int32)

    table = jnp.concatenate([neighbours, counts[:, None]], axis=1).astype(jnp.float32)
    all_table = lax.all_gather(table, "ctx", axis=0, tiled=True).astype(jnp.int32)
    all_table = all_table.reshape(n_ctx, tile_count, KMAX + 1)
    all_live = jnp.arange(KMAX)[None, None, :] < all_table[:, :, KMAX:]
    send_first, send_second = first_two(
        all_table[:, :, :KMAX], all_live, jnp.full((n_ctx,), own_index), tile_count
    )
    send_picks = jnp.stack([send_first, send_second], axis=1).reshape(-1)

    live = jnp.arange(KMAX)[None, :] < counts[:, None]
    recv_first, _ = first_two(
        jnp.broadcast_to(neighbours[None], (n_ctx,) + neighbours.shape),
        jnp.broadcast_to(live[None], (n_ctx,) + live.shape),
        devices,
        tile_count,
    )
    source = neighbours // tile_count
    within = neighbours % tile_count
    remote_slot = tile_count + CAP * source + jnp.where(within == recv_first[source], 0, 1)
    positions = jnp.where(source == own_index, within, remote_slot).astype(jnp.int32)
    bias = jnp.transpose(jnp.take(rel_bias, bias_index, axis=1), (1, 0, 2))
    live_counts = counts.astype(jnp.int32)

    own_tokens = clip_tokens[0]
    order = [1, 3, 2, 0] if n_dp == 4 else list(range(1, n_dp)) + [0]
    arrived = {0: own_tokens}
    for step in range(1, n_dp):
        arrived[step] = lax.ppermute(own_tokens, "dp", partner_pairs(n_dp, step))
    total = None
    received = []
    partials = []
    sent = []
    for index, step in enumerate(order):
        tokens = arrived[step]
        if index >= 1:
            tokens, _ = lax.optimization_barrier((tokens, received[max(index - 2, 0)]))
        projected = jnp.einsum(
            "td,sdh->sth", tokens, qkv_weight, preferred_element_type=jnp.float32
        ).astype(jnp.bfloat16)
        queries = projected[0][None]
        by_tile = jnp.transpose(
            projected[1:3].reshape(2, tile_count, TILE, width_here), (1, 0, 2, 3)
        )[:, :, None]
        payload = jnp.take(by_tile, send_picks, axis=0)
        if index >= 2:
            payload, _ = lax.optimization_barrier((payload, partials[index - 2]))
        if index == len(order) - 1 and len(sent) >= 2:
            payload, _ = lax.optimization_barrier((payload, sent[-3]))
        incoming = lax.all_to_all(payload, "ctx", 0, 0, tiled=True)
        received.append(incoming)
        key_values = jnp.concatenate([by_tile, incoming], axis=0)
        if index == len(order) - 1 and len(sent) >= 2:
            key_values, _ = lax.optimization_barrier((key_values, sent[-2]))
        attended = attend(positions, live_counts, bias, queries, key_values, heads_here, head_size)
        partial_out = jnp.dot(
            attended[0], out_weight, preferred_element_type=jnp.float32
        ).astype(jnp.bfloat16)
        partials.append(partial_out)
        if step > 0:
            partial_out = lax.ppermute(partial_out, "dp", partner_pairs(n_dp, step))
            sent.append(partial_out)
        contribution = partial_out.astype(jnp.float32)
        total = contribution if total is None else total + contribution
    return total.astype(jnp.bfloat16)[None]


def solution(mesh):
    placed = (
        P("dp", "ctx", None),
        P(None, None, "dp"),
        P("dp", None),
        P("ctx", None),
        P("ctx"),
        P("ctx", None),
        P("dp", None),
    )
    return jax.shard_map(
        local, mesh=mesh, in_specs=placed, out_specs=P("dp", "ctx", None), check_vma=False
    )
```

```python
import functools
import math

import jax
import jax.numpy as jnp
from jax import lax
from jax.experimental import pallas as pl
from jax.experimental.pallas import tpu as pltpu
from jax.sharding import PartitionSpec as P

TILE = 64
REACH = 6
KMAX = 10
CAP = 2


def first_two(rows, rows_live, sources, tiles_per_device):
    local = jnp.arange(tiles_per_device, dtype=jnp.int32)
    wanted = sources[:, None] * tiles_per_device + local[None, :]
    named = jnp.any(
        (rows[:, :, :, None] == wanted[:, None, None, :]) & rows_live[:, :, :, None], axis=(1, 2)
    )
    order = jnp.where(named, local[None, :], tiles_per_device)
    first = jnp.min(order, axis=1)
    second = jnp.min(jnp.where(order > first[:, None], order, tiles_per_device), axis=1)
    first = jnp.where(first == tiles_per_device, 0, first)
    second = jnp.where(second == tiles_per_device, 0, second)
    return first.astype(jnp.int32), second.astype(jnp.int32)


def attention_kernel(pos_ref, count_ref, bias_ref, q_ref, *refs, heads, head_size, scale):
    kv_refs = refs[:KMAX]
    out_ref = refs[KMAX]
    tile = pl.program_id(0)
    live_count = count_ref[tile]
    queries = q_ref[...]
    clip_count = queries.shape[0]
    for head in range(heads):
        cols = slice(head * head_size, (head + 1) * head_size)
        q_head = queries[:, :, cols]
        scores = []
        for slot in range(KMAX):
            k_head = kv_refs[slot][0, :, :, cols]
            s = lax.dot_general(
                q_head, k_head, (((2,), (2,)), ((0,), (0,))), preferred_element_type=jnp.float32
            )
            s = s * scale + bias_ref[tile, head, slot]
            s = jnp.where(slot < live_count, s, -1e30)
            scores.append(s)
        row_max = scores[0].max(axis=2, keepdims=True)
        for s in scores[1:]:
            row_max = jnp.maximum(row_max, s.max(axis=2, keepdims=True))
        total = jnp.zeros((clip_count, TILE, head_size), jnp.float32)
        weight_sum = jnp.zeros((clip_count, TILE, 1), jnp.float32)
        for slot in range(KMAX):
            w = jnp.exp(scores[slot] - row_max)
            weight_sum = weight_sum + w.sum(axis=2, keepdims=True)
            v_head = kv_refs[slot][1, :, :, cols]
            total = total + lax.dot_general(
                w.astype(jnp.bfloat16), v_head, (((2,), (1,)), ((0,), (0,))),
                preferred_element_type=jnp.float32,
            )
        out_ref[:, :, cols] = (total / weight_sum).astype(out_ref.dtype)


def attend(positions, live_counts, bias, queries, key_values, heads, head_size):
    clip_count, token_count, width = queries.shape
    tile_count = token_count // TILE

    def kv_spec(slot):
        return pl.BlockSpec(
            (None, 2, clip_count, TILE, width),
            lambda t, pos, cnt, slot=slot: (pos[t, slot], 0, 0, 0, 0),
        )

    kernel = functools.partial(
        attention_kernel, heads=heads, head_size=head_size, scale=1.0 / math.sqrt(head_size)
    )
    return pl.pallas_call(
        kernel,
        out_shape=jax.ShapeDtypeStruct(queries.shape, jnp.bfloat16),
        grid_spec=pltpu.PrefetchScalarGridSpec(
            num_scalar_prefetch=2,
            grid=(tile_count,),
            in_specs=[pl.BlockSpec(memory_space=pltpu.SMEM),
                      pl.BlockSpec((clip_count, TILE, width), lambda t, pos, cnt: (0, t, 0))]
            + [kv_spec(slot) for slot in range(KMAX)],
            out_specs=pl.BlockSpec((clip_count, TILE, width), lambda t, pos, cnt: (0, t, 0)),
        ),
    )(positions, live_counts, bias, queries, *([key_values] * KMAX))


def partner_pairs(count, step):
    return [(source, source ^ step) for source in range(count)]


def local(clip_tokens, qkv_weight, out_weight, neighbours, counts, bias_index, rel_bias):
    heads_here = rel_bias.shape[0]
    width_here = out_weight.shape[0]
    head_size = width_here // heads_here
    token_count = clip_tokens.shape[1]
    tile_count = token_count // TILE
    n_ctx = lax.axis_size("ctx")
    n_dp = lax.axis_size("dp")
    own_index = lax.axis_index("ctx").astype(jnp.int32)
    devices = jnp.arange(n_ctx, dtype=jnp.int32)

    table = jnp.concatenate([neighbours, counts[:, None]], axis=1).astype(jnp.float32)
    all_table = lax.all_gather(table, "ctx", axis=0, tiled=True).astype(jnp.int32)
    all_table = all_table.reshape(n_ctx, tile_count, KMAX + 1)
    all_live = jnp.arange(KMAX)[None, None, :] < all_table[:, :, KMAX:]
    send_first, send_second = first_two(
        all_table[:, :, :KMAX], all_live, jnp.full((n_ctx,), own_index), tile_count
    )
    send_picks = jnp.stack([send_first, send_second], axis=1).reshape(-1)

    live = jnp.arange(KMAX)[None, :] < counts[:, None]
    recv_first, _ = first_two(
        jnp.broadcast_to(neighbours[None], (n_ctx,) + neighbours.shape),
        jnp.broadcast_to(live[None], (n_ctx,) + live.shape),
        devices,
        tile_count,
    )
    source = neighbours // tile_count
    within = neighbours % tile_count
    remote_slot = tile_count + CAP * source + jnp.where(within == recv_first[source], 0, 1)
    positions = jnp.where(source == own_index, within, remote_slot).astype(jnp.int32)
    bias = jnp.transpose(jnp.take(rel_bias, bias_index, axis=1), (1, 0, 2))
    live_counts = counts.astype(jnp.int32)

    own_tokens = clip_tokens[0]
    order = [3, 1, 2, 0] if n_dp == 4 else list(range(1, n_dp)) + [0]
    arrived = {0: own_tokens}
    for step in range(1, n_dp):
        arrived[step] = lax.ppermute(own_tokens, "dp", partner_pairs(n_dp, step))
    total = None
    received = []
    partials = []
    sent = []
    for index, step in enumerate(order):
        tokens = arrived[step]
        if index >= 1:
            tokens, _ = lax.optimization_barrier((tokens, received[max(index - 2, 0)]))
        projected = jnp.einsum(
            "td,sdh->sth", tokens, qkv_weight, preferred_element_type=jnp.float32
        ).astype(jnp.bfloat16)
        queries = projected[0][None]
        by_tile = jnp.transpose(
            projected[1:3].reshape(2, tile_count, TILE, width_here), (1, 0, 2, 3)
        )[:, :, None]
        payload = jnp.take(by_tile, send_picks, axis=0)
        if index >= 2:
            payload, _ = lax.optimization_barrier((payload, partials[index - 2]))
        if index == len(order) - 1 and len(sent) >= 2:
            payload, _ = lax.optimization_barrier((payload, sent[-3]))
        incoming = lax.all_to_all(payload, "ctx", 0, 0, tiled=True)
        received.append(incoming)
        key_values = jnp.concatenate([by_tile, incoming], axis=0)
        if index == len(order) - 1 and len(sent) >= 2:
            key_values, _ = lax.optimization_barrier((key_values, sent[-2]))
        attended = attend(positions, live_counts, bias, queries, key_values, heads_here, head_size)
        partial_out = jnp.dot(
            attended[0], out_weight, preferred_element_type=jnp.float32
        ).astype(jnp.bfloat16)
        partials.append(partial_out)
        if step > 0:
            partial_out = lax.ppermute(partial_out, "dp", partner_pairs(n_dp, step))
            sent.append(partial_out)
        contribution = partial_out.astype(jnp.float32)
        total = contribution if total is None else total + contribution
    return total.astype(jnp.bfloat16)[None]


def solution(mesh):
    placed = (
        P("dp", "ctx", None),
        P(None, None, "dp"),
        P("dp", None),
        P("ctx", None),
        P("ctx"),
        P("ctx", None),
        P("dp", None),
    )
    return jax.shard_map(
        local, mesh=mesh, in_specs=placed, out_specs=P("dp", "ctx", None), check_vma=False
    )
```

```python
import functools
import math

import jax
import jax.numpy as jnp
from jax import lax
from jax.experimental import pallas as pl
from jax.experimental.pallas import tpu as pltpu
from jax.sharding import PartitionSpec as P

TILE = 64
REACH = 6
KMAX = 10
CAP = 2


def first_two(rows, rows_live, sources, tiles_per_device):
    local = jnp.arange(tiles_per_device, dtype=jnp.int32)
    wanted = sources[:, None] * tiles_per_device + local[None, :]
    named = jnp.any(
        (rows[:, :, :, None] == wanted[:, None, None, :]) & rows_live[:, :, :, None], axis=(1, 2)
    )
    order = jnp.where(named, local[None, :], tiles_per_device)
    first = jnp.min(order, axis=1)
    second = jnp.min(jnp.where(order > first[:, None], order, tiles_per_device), axis=1)
    first = jnp.where(first == tiles_per_device, 0, first)
    second = jnp.where(second == tiles_per_device, 0, second)
    return first.astype(jnp.int32), second.astype(jnp.int32)


def attention_kernel(pos_ref, count_ref, bias_ref, q_ref, *refs, heads, head_size, scale):
    kv_refs = refs[:KMAX]
    out_ref = refs[KMAX]
    tile = pl.program_id(0)
    live_count = count_ref[tile]
    queries = q_ref[...]
    clip_count = queries.shape[0]
    for head in range(heads):
        cols = slice(head * head_size, (head + 1) * head_size)
        q_head = queries[:, :, cols]
        scores = []
        for slot in range(KMAX):
            k_head = kv_refs[slot][0, :, :, cols]
            s = lax.dot_general(
                q_head, k_head, (((2,), (2,)), ((0,), (0,))), preferred_element_type=jnp.float32
            )
            s = s * scale + bias_ref[tile, head, slot]
            s = jnp.where(slot < live_count, s, -1e30)
            scores.append(s)
        row_max = scores[0].max(axis=2, keepdims=True)
        for s in scores[1:]:
            row_max = jnp.maximum(row_max, s.max(axis=2, keepdims=True))
        total = jnp.zeros((clip_count, TILE, head_size), jnp.float32)
        weight_sum = jnp.zeros((clip_count, TILE, 1), jnp.float32)
        for slot in range(KMAX):
            w = jnp.exp(scores[slot] - row_max)
            weight_sum = weight_sum + w.sum(axis=2, keepdims=True)
            v_head = kv_refs[slot][1, :, :, cols]
            total = total + lax.dot_general(
                w.astype(jnp.bfloat16), v_head, (((2,), (1,)), ((0,), (0,))),
                preferred_element_type=jnp.float32,
            )
        out_ref[:, :, cols] = (total / weight_sum).astype(out_ref.dtype)


def attend(positions, live_counts, bias, queries, key_values, heads, head_size):
    _, token_count, width = queries.shape
    clip_count = 1
    tile_count = token_count // TILE

    def kv_spec(slot):
        return pl.BlockSpec(
            (None, 2, clip_count, TILE, width),
            lambda t, pos, cnt, slot=slot: (pos[t, slot], 0, 0, 0, 0),
        )

    kernel = functools.partial(
        attention_kernel, heads=heads, head_size=head_size, scale=1.0 / math.sqrt(head_size)
    )
    return pl.pallas_call(
        kernel,
        out_shape=jax.ShapeDtypeStruct((clip_count, token_count, width), jnp.bfloat16),
        grid_spec=pltpu.PrefetchScalarGridSpec(
            num_scalar_prefetch=2,
            grid=(tile_count,),
            in_specs=[pl.BlockSpec(memory_space=pltpu.SMEM),
                      pl.BlockSpec((clip_count, TILE, width), lambda t, pos, cnt: (0, t, 0))]
            + [kv_spec(slot) for slot in range(KMAX)],
            out_specs=pl.BlockSpec((clip_count, TILE, width), lambda t, pos, cnt: (0, t, 0)),
        ),
    )(positions, live_counts, bias, queries, *([key_values] * KMAX))


def partner_pairs(count, step):
    return [(source, source ^ step) for source in range(count)]


def local(clip_tokens, qkv_weight, out_weight, neighbours, counts, bias_index, rel_bias):
    heads_here = rel_bias.shape[0]
    width_here = out_weight.shape[0]
    head_size = width_here // heads_here
    token_count = clip_tokens.shape[1]
    tile_count = token_count // TILE
    n_ctx = lax.axis_size("ctx")
    n_dp = lax.axis_size("dp")
    own_index = lax.axis_index("ctx").astype(jnp.int32)
    devices = jnp.arange(n_ctx, dtype=jnp.int32)

    table = jnp.concatenate([neighbours, counts[:, None]], axis=1).astype(jnp.float32)
    all_table = lax.all_gather(table, "ctx", axis=0, tiled=True).astype(jnp.int32)
    all_table = all_table.reshape(n_ctx, tile_count, KMAX + 1)
    all_live = jnp.arange(KMAX)[None, None, :] < all_table[:, :, KMAX:]
    send_first, send_second = first_two(
        all_table[:, :, :KMAX], all_live, jnp.full((n_ctx,), own_index), tile_count
    )
    send_picks = jnp.stack([send_first, send_second], axis=1).reshape(-1)

    live = jnp.arange(KMAX)[None, :] < counts[:, None]
    recv_first, _ = first_two(
        jnp.broadcast_to(neighbours[None], (n_ctx,) + neighbours.shape),
        jnp.broadcast_to(live[None], (n_ctx,) + live.shape),
        devices,
        tile_count,
    )
    source = neighbours // tile_count
    within = neighbours % tile_count
    remote_slot = tile_count + CAP * source + jnp.where(within == recv_first[source], 0, 1)
    positions = jnp.where(source == own_index, within, remote_slot).astype(jnp.int32)
    bias = jnp.transpose(jnp.take(rel_bias, bias_index, axis=1), (1, 0, 2))
    live_counts = counts.astype(jnp.int32)

    own_tokens = clip_tokens[0]
    order = [3, 1, 2, 0] if n_dp == 4 else list(range(1, n_dp)) + [0]
    arrived = {0: own_tokens}
    for step in range(1, n_dp):
        arrived[step] = lax.ppermute(own_tokens, "dp", partner_pairs(n_dp, step))
    total = None
    received = []
    partials = []
    sent = []
    for index, step in enumerate(order):
        tokens = arrived[step]
        if index >= 1:
            tokens, _ = lax.optimization_barrier((tokens, received[max(index - 2, 0)]))
        projected = jnp.einsum(
            "td,sdh->sth", tokens, qkv_weight, preferred_element_type=jnp.float32
        ).astype(jnp.bfloat16)
        by_tile = jnp.transpose(
            projected[1:3].reshape(2, tile_count, TILE, width_here), (1, 0, 2, 3)
        )[:, :, None]
        payload = by_tile.at[send_picks].get(mode="promise_in_bounds")
        if index >= 2:
            payload, _ = lax.optimization_barrier((payload, partials[index - 2]))
        if index == len(order) - 1 and len(sent) >= 2:
            payload, _ = lax.optimization_barrier((payload, sent[-3]))
        incoming = lax.all_to_all(payload, "ctx", 0, 0, tiled=True)
        received.append(incoming)
        key_values = jnp.concatenate([by_tile, incoming], axis=0)
        if index == len(order) - 1 and len(sent) >= 2:
            key_values, _ = lax.optimization_barrier((key_values, sent[-2]))
        attended = attend(positions, live_counts, bias, projected, key_values, heads_here, head_size)
        partial_out = jnp.dot(
            attended[0], out_weight, preferred_element_type=jnp.float32
        ).astype(jnp.bfloat16)
        partials.append(partial_out)
        if step > 0:
            partial_out = lax.ppermute(partial_out, "dp", partner_pairs(n_dp, step))
            sent.append(partial_out)
        contribution = partial_out.astype(jnp.float32)
        total = contribution if total is None else total + contribution
    return total.astype(jnp.bfloat16)[None]


def solution(mesh):
    placed = (
        P("dp", "ctx", None),
        P(None, None, "dp"),
        P("dp", None),
        P("ctx", None),
        P("ctx"),
        P("ctx", None),
        P("dp", None),
    )
    return jax.shard_map(
        local, mesh=mesh, in_specs=placed, out_specs=P("dp", "ctx", None), check_vma=False
    )
```

```python
import functools
import math

import jax
import jax.numpy as jnp
from jax import lax
from jax.experimental import pallas as pl
from jax.experimental.pallas import tpu as pltpu
from jax.sharding import PartitionSpec as P

TILE = 64
REACH = 6
KMAX = 10
CAP = 2


def first_two(rows, rows_live, sources, tiles_per_device):
    local = jnp.arange(tiles_per_device, dtype=jnp.int32)
    wanted = sources[:, None] * tiles_per_device + local[None, :]
    named = jnp.any(
        (rows[:, :, :, None] == wanted[:, None, None, :]) & rows_live[:, :, :, None], axis=(1, 2)
    )
    order = jnp.where(named, local[None, :], tiles_per_device)
    first = jnp.min(order, axis=1)
    second = jnp.min(jnp.where(order > first[:, None], order, tiles_per_device), axis=1)
    first = jnp.where(first == tiles_per_device, 0, first)
    second = jnp.where(second == tiles_per_device, 0, second)
    return first.astype(jnp.int32), second.astype(jnp.int32)


def attention_kernel(pos_ref, count_ref, bias_ref, q_ref, *refs, heads, head_size, scale):
    kv_refs = refs[:KMAX]
    out_ref = refs[KMAX]
    tile = pl.program_id(0)
    live_count = count_ref[tile]
    queries = q_ref[...]
    clip_count = queries.shape[0]
    for head in range(heads):
        cols = slice(head * head_size, (head + 1) * head_size)
        q_head = queries[:, :, cols]
        scores = []
        for slot in range(KMAX):
            k_head = kv_refs[slot][0, :, :, cols]
            s = lax.dot_general(
                q_head, k_head, (((2,), (2,)), ((0,), (0,))), preferred_element_type=jnp.float32
            )
            s = s * scale + bias_ref[tile, head, slot]
            s = jnp.where(slot < live_count, s, -1e30)
            scores.append(s)
        row_max = scores[0].max(axis=2, keepdims=True)
        for s in scores[1:]:
            row_max = jnp.maximum(row_max, s.max(axis=2, keepdims=True))
        total = jnp.zeros((clip_count, TILE, head_size), jnp.float32)
        weight_sum = jnp.zeros((clip_count, TILE, 1), jnp.float32)
        for slot in range(KMAX):
            w = jnp.exp(scores[slot] - row_max)
            weight_sum = weight_sum + w.sum(axis=2, keepdims=True)
            v_head = kv_refs[slot][1, :, :, cols]
            total = total + lax.dot_general(
                w.astype(jnp.bfloat16), v_head, (((2,), (1,)), ((0,), (0,))),
                preferred_element_type=jnp.float32,
            )
        out_ref[:, :, cols] = (total / weight_sum).astype(out_ref.dtype)


def attend(positions, live_counts, bias, queries, key_values, heads, head_size):
    _, token_count, width = queries.shape
    clip_count = 1
    tile_count = token_count // TILE

    def kv_spec(slot):
        return pl.BlockSpec(
            (None, 2, clip_count, TILE, width),
            lambda t, pos, cnt, slot=slot: (pos[t, slot], 0, 0, 0, 0),
        )

    kernel = functools.partial(
        attention_kernel, heads=heads, head_size=head_size, scale=1.0 / math.sqrt(head_size)
    )
    return pl.pallas_call(
        kernel,
        out_shape=jax.ShapeDtypeStruct((clip_count, token_count, width), jnp.bfloat16),
        grid_spec=pltpu.PrefetchScalarGridSpec(
            num_scalar_prefetch=2,
            grid=(tile_count,),
            in_specs=[pl.BlockSpec(memory_space=pltpu.SMEM),
                      pl.BlockSpec((clip_count, TILE, width), lambda t, pos, cnt: (0, t, 0))]
            + [kv_spec(slot) for slot in range(KMAX)],
            out_specs=pl.BlockSpec((clip_count, TILE, width), lambda t, pos, cnt: (0, t, 0)),
        ),
    )(positions, live_counts, bias, queries, *([key_values] * KMAX))


def partner_pairs(count, step):
    return [(source, source ^ step) for source in range(count)]


def local(clip_tokens, qkv_weight, out_weight, neighbours, counts, bias_index, rel_bias):
    heads_here = rel_bias.shape[0]
    width_here = out_weight.shape[0]
    head_size = width_here // heads_here
    token_count = clip_tokens.shape[1]
    tile_count = token_count // TILE
    n_ctx = lax.axis_size("ctx")
    n_dp = lax.axis_size("dp")
    own_index = lax.axis_index("ctx").astype(jnp.int32)
    devices = jnp.arange(n_ctx, dtype=jnp.int32)

    table = jnp.concatenate([neighbours, counts[:, None]], axis=1).astype(jnp.float32)
    all_table = lax.all_gather(table, "ctx", axis=0, tiled=True).astype(jnp.int32)
    all_table = all_table.reshape(n_ctx, tile_count, KMAX + 1)
    all_live = jnp.arange(KMAX)[None, None, :] < all_table[:, :, KMAX:]
    send_first, send_second = first_two(
        all_table[:, :, :KMAX], all_live, jnp.full((n_ctx,), own_index), tile_count
    )
    send_picks = jnp.stack([send_first, send_second], axis=1).reshape(-1)

    live = jnp.arange(KMAX)[None, :] < counts[:, None]
    recv_first, _ = first_two(
        jnp.broadcast_to(neighbours[None], (n_ctx,) + neighbours.shape),
        jnp.broadcast_to(live[None], (n_ctx,) + live.shape),
        devices,
        tile_count,
    )
    source = neighbours // tile_count
    within = neighbours % tile_count
    remote_slot = tile_count + CAP * source + jnp.where(within == recv_first[source], 0, 1)
    positions = jnp.where(source == own_index, within, remote_slot).astype(jnp.int32)
    bias = jnp.transpose(jnp.take(rel_bias, bias_index, axis=1), (1, 0, 2))
    live_counts = counts.astype(jnp.int32)

    own_tokens = clip_tokens[0]
    order = [0, 3, 1, 2] if n_dp == 4 else list(range(n_dp))
    arrived = {0: own_tokens}
    for step in range(1, n_dp):
        arrived[step] = lax.ppermute(own_tokens, "dp", partner_pairs(n_dp, step))
    last = order[-1]
    if last > 0:
        far_weight = lax.ppermute(out_weight, "dp", partner_pairs(n_dp, last))
    total = None
    received = []
    partials = []
    sent = []
    for index, step in enumerate(order):
        final = index == len(order) - 1
        tokens = arrived[step]
        if index >= 1:
            tokens, _ = lax.optimization_barrier((tokens, received[max(index - 2, 0)]))
        projected = jnp.einsum(
            "td,sdh->sth", tokens, qkv_weight, preferred_element_type=jnp.float32
        ).astype(jnp.bfloat16)
        by_tile = jnp.transpose(
            projected[1:3].reshape(2, tile_count, TILE, width_here), (1, 0, 2, 3)
        )[:, :, None]
        payload = by_tile.at[send_picks].get(mode="promise_in_bounds")
        if index >= 2:
            payload, _ = lax.optimization_barrier((payload, partials[index - 2]))
        if final and last > 0:
            payload, far_weight = lax.optimization_barrier((payload, far_weight))
        if final and len(sent) >= 2:
            payload, _ = lax.optimization_barrier((payload, sent[-2]))
        incoming = lax.all_to_all(payload, "ctx", 0, 0, tiled=True)
        received.append(incoming)
        key_values = jnp.concatenate([by_tile, incoming], axis=0)
        if final and len(sent) >= 1:
            key_values, _ = lax.optimization_barrier((key_values, sent[-1]))
        attended = attend(positions, live_counts, bias, projected, key_values, heads_here, head_size)
        if final and step > 0:
            came = lax.ppermute(attended[0], "dp", partner_pairs(n_dp, step))
            partial_out = jnp.dot(
                came, far_weight, preferred_element_type=jnp.float32
            ).astype(jnp.bfloat16)
        else:
            partial_out = jnp.dot(
                attended[0], out_weight, preferred_element_type=jnp.float32
            ).astype(jnp.bfloat16)
            partials.append(partial_out)
            if step > 0:
                partial_out = lax.ppermute(partial_out, "dp", partner_pairs(n_dp, step))
                sent.append(partial_out)
        contribution = partial_out.astype(jnp.float32)
        total = contribution if total is None else total + contribution
    return total.astype(jnp.bfloat16)[None]


def solution(mesh):
    placed = (
        P("dp", "ctx", None),
        P(None, None, "dp"),
        P("dp", None),
        P("ctx", None),
        P("ctx"),
        P("ctx", None),
        P("dp", None),
    )
    return jax.shard_map(
        local, mesh=mesh, in_specs=placed, out_specs=P("dp", "ctx", None), check_vma=False
    )
```

```python
import functools
import math

import jax
import jax.numpy as jnp
from jax import lax
from jax.experimental import pallas as pl
from jax.experimental.pallas import tpu as pltpu
from jax.sharding import PartitionSpec as P

TILE = 64
REACH = 6
KMAX = 10
CAP = 2


def first_two(rows, rows_live, sources, tiles_per_device):
    local = jnp.arange(tiles_per_device, dtype=jnp.int32)
    wanted = sources[:, None] * tiles_per_device + local[None, :]
    named = jnp.any(
        (rows[:, :, :, None] == wanted[:, None, None, :]) & rows_live[:, :, :, None], axis=(1, 2)
    )
    order = jnp.where(named, local[None, :], tiles_per_device)
    first = jnp.min(order, axis=1)
    second = jnp.min(jnp.where(order > first[:, None], order, tiles_per_device), axis=1)
    first = jnp.where(first == tiles_per_device, 0, first)
    second = jnp.where(second == tiles_per_device, 0, second)
    return first.astype(jnp.int32), second.astype(jnp.int32)


def attention_kernel(pos_ref, count_ref, bias_ref, q_ref, *refs, heads, head_size, scale):
    kv_refs = refs[:KMAX]
    out_ref = refs[KMAX]
    tile = pl.program_id(0)
    live_count = count_ref[tile]
    queries = q_ref[...]
    clip_count = queries.shape[0]
    for head in range(heads):
        cols = slice(head * head_size, (head + 1) * head_size)
        q_head = queries[:, :, cols]
        scores = []
        for slot in range(KMAX):
            k_head = kv_refs[slot][0, :, :, cols]
            s = lax.dot_general(
                q_head, k_head, (((2,), (2,)), ((0,), (0,))), preferred_element_type=jnp.float32
            )
            s = s * scale + bias_ref[tile, head, slot]
            s = jnp.where(slot < live_count, s, -1e30)
            scores.append(s)
        row_max = scores[0].max(axis=2, keepdims=True)
        for s in scores[1:]:
            row_max = jnp.maximum(row_max, s.max(axis=2, keepdims=True))
        total = jnp.zeros((clip_count, TILE, head_size), jnp.float32)
        weight_sum = jnp.zeros((clip_count, TILE, 1), jnp.float32)
        for slot in range(KMAX):
            w = jnp.exp(scores[slot] - row_max)
            weight_sum = weight_sum + w.sum(axis=2, keepdims=True)
            v_head = kv_refs[slot][1, :, :, cols]
            total = total + lax.dot_general(
                w.astype(jnp.bfloat16), v_head, (((2,), (1,)), ((0,), (0,))),
                preferred_element_type=jnp.float32,
            )
        out_ref[:, :, cols] = (total / weight_sum).astype(out_ref.dtype)


def attend(positions, live_counts, bias, queries, key_values, heads, head_size):
    _, token_count, width = queries.shape
    clip_count = 1
    tile_count = token_count // TILE

    def kv_spec(slot):
        return pl.BlockSpec(
            (None, 2, clip_count, TILE, width),
            lambda t, pos, cnt, slot=slot: (pos[t, slot], 0, 0, 0, 0),
        )

    kernel = functools.partial(
        attention_kernel, heads=heads, head_size=head_size, scale=1.0 / math.sqrt(head_size)
    )
    return pl.pallas_call(
        kernel,
        out_shape=jax.ShapeDtypeStruct((clip_count, token_count, width), jnp.bfloat16),
        grid_spec=pltpu.PrefetchScalarGridSpec(
            num_scalar_prefetch=2,
            grid=(tile_count,),
            in_specs=[pl.BlockSpec(memory_space=pltpu.SMEM),
                      pl.BlockSpec((clip_count, TILE, width), lambda t, pos, cnt: (0, t, 0))]
            + [kv_spec(slot) for slot in range(KMAX)],
            out_specs=pl.BlockSpec((clip_count, TILE, width), lambda t, pos, cnt: (0, t, 0)),
        ),
    )(positions, live_counts, bias, queries, *([key_values] * KMAX))


def partner_pairs(count, step):
    return [(source, source ^ step) for source in range(count)]


def local(clip_tokens, qkv_weight, out_weight, neighbours, counts, bias_index, rel_bias):
    heads_here = rel_bias.shape[0]
    width_here = out_weight.shape[0]
    head_size = width_here // heads_here
    token_count = clip_tokens.shape[1]
    tile_count = token_count // TILE
    n_ctx = lax.axis_size("ctx")
    n_dp = lax.axis_size("dp")
    own_index = lax.axis_index("ctx").astype(jnp.int32)
    devices = jnp.arange(n_ctx, dtype=jnp.int32)

    table = jnp.concatenate([neighbours, counts[:, None]], axis=1).astype(jnp.float32)
    all_table = lax.all_gather(table, "ctx", axis=0, tiled=True).astype(jnp.int32)
    all_table = all_table.reshape(n_ctx, tile_count, KMAX + 1)
    all_live = jnp.arange(KMAX)[None, None, :] < all_table[:, :, KMAX:]
    send_first, send_second = first_two(
        all_table[:, :, :KMAX], all_live, jnp.full((n_ctx,), own_index), tile_count
    )
    send_picks = jnp.stack([send_first, send_second], axis=1).reshape(-1)

    live = jnp.arange(KMAX)[None, :] < counts[:, None]
    recv_first, _ = first_two(
        jnp.broadcast_to(neighbours[None], (n_ctx,) + neighbours.shape),
        jnp.broadcast_to(live[None], (n_ctx,) + live.shape),
        devices,
        tile_count,
    )
    source = neighbours // tile_count
    within = neighbours % tile_count
    remote_slot = tile_count + CAP * source + jnp.where(within == recv_first[source], 0, 1)
    positions = jnp.where(source == own_index, within, remote_slot).astype(jnp.int32)
    bias = jnp.transpose(jnp.take(rel_bias, bias_index, axis=1), (1, 0, 2))
    live_counts = counts.astype(jnp.int32)

    own_tokens = clip_tokens[0]
    order = [3, 1, 2, 0] if n_dp == 4 else list(range(1, n_dp)) + [0]
    arrived = {0: own_tokens}
    for step in range(1, n_dp):
        arrived[step] = lax.ppermute(own_tokens, "dp", partner_pairs(n_dp, step))
    total = None
    received = []
    partials = []
    sent = []
    for index, step in enumerate(order):
        tokens = arrived[step]
        if index >= 1:
            tokens, _ = lax.optimization_barrier((tokens, received[max(index - 2, 0)]))
        projected = jnp.einsum(
            "td,sdh->sth", tokens, qkv_weight, preferred_element_type=jnp.float32
        ).astype(jnp.bfloat16)
        by_tile = jnp.transpose(
            projected[1:3].reshape(2, tile_count, TILE, width_here), (1, 0, 2, 3)
        )[:, :, None]
        payload = by_tile.at[send_picks].get(mode="promise_in_bounds")
        if index >= 2:
            payload, _ = lax.optimization_barrier((payload, partials[index - 2]))
        if index == len(order) - 1 and len(sent) >= 2:
            payload, _ = lax.optimization_barrier((payload, sent[-3]))
        incoming = jnp.concatenate(
            [lax.all_to_all(payload[:, part:part + 1], "ctx", 0, 0, tiled=True) for part in range(2)],
            axis=1,
        )
        received.append(incoming)
        key_values = jnp.concatenate([by_tile, incoming], axis=0)
        if index == len(order) - 1 and len(sent) >= 2:
            key_values, _ = lax.optimization_barrier((key_values, sent[-2]))
        attended = attend(positions, live_counts, bias, projected, key_values, heads_here, head_size)
        partial_out = jnp.dot(
            attended[0], out_weight, preferred_element_type=jnp.float32
        ).astype(jnp.bfloat16)
        partials.append(partial_out)
        if step > 0:
            partial_out = lax.ppermute(partial_out, "dp", partner_pairs(n_dp, step))
            sent.append(partial_out)
        contribution = partial_out.astype(jnp.float32)
        total = contribution if total is None else total + contribution
    return total.astype(jnp.bfloat16)[None]


def solution(mesh):
    placed = (
        P("dp", "ctx", None),
        P(None, None, "dp"),
        P("dp", None),
        P("ctx", None),
        P("ctx"),
        P("ctx", None),
        P("dp", None),
    )
    return jax.shard_map(
        local, mesh=mesh, in_specs=placed, out_specs=P("dp", "ctx", None), check_vma=False
    )
```

```python
import functools
import math

import jax
import jax.numpy as jnp
from jax import lax
from jax.experimental import pallas as pl
from jax.experimental.pallas import tpu as pltpu
from jax.sharding import PartitionSpec as P

TILE = 64
REACH = 6
KMAX = 10
CAP = 2


def first_two(rows, rows_live, sources, tiles_per_device):
    local = jnp.arange(tiles_per_device, dtype=jnp.int32)
    wanted = sources[:, None] * tiles_per_device + local[None, :]
    named = jnp.any(
        (rows[:, :, :, None] == wanted[:, None, None, :]) & rows_live[:, :, :, None], axis=(1, 2)
    )
    order = jnp.where(named, local[None, :], tiles_per_device)
    first = jnp.min(order, axis=1)
    second = jnp.min(jnp.where(order > first[:, None], order, tiles_per_device), axis=1)
    first = jnp.where(first == tiles_per_device, 0, first)
    second = jnp.where(second == tiles_per_device, 0, second)
    return first.astype(jnp.int32), second.astype(jnp.int32)


def attention_kernel(pos_ref, count_ref, bias_ref, q_ref, own_ref, far_ref, out_ref, *, heads, head_size, scale):
    tile = pl.program_id(0)
    own_tiles = own_ref.shape[0]
    live_count = count_ref[tile]
    queries = q_ref[0]
    picks = []
    for slot in range(KMAX):
        where = pos_ref[tile, slot]
        picks.append((
            where < own_tiles,
            jnp.minimum(where, own_tiles - 1),
            jnp.maximum(where - own_tiles, 0),
        ))

    def rows(part, slot, cols):
        mine, near, far = picks[slot]
        return jnp.where(mine, own_ref[near, part, 0, :, cols], far_ref[far, part, 0, :, cols])

    for head in range(heads):
        cols = pl.ds(head * head_size, head_size)
        q_head = queries[:, head * head_size:(head + 1) * head_size]
        scores = []
        for slot in range(KMAX):
            s = lax.dot_general(
                q_head, rows(0, slot, cols), (((1,), (1,)), ((), ())),
                preferred_element_type=jnp.float32,
            )
            s = s * scale + bias_ref[tile, head, slot]
            s = jnp.where(slot < live_count, s, -1e30)
            scores.append(s)
        row_max = scores[0].max(axis=1, keepdims=True)
        for s in scores[1:]:
            row_max = jnp.maximum(row_max, s.max(axis=1, keepdims=True))
        total = jnp.zeros((TILE, head_size), jnp.float32)
        weight_sum = jnp.zeros((TILE, 1), jnp.float32)
        for slot in range(KMAX):
            w = jnp.exp(scores[slot] - row_max)
            weight_sum = weight_sum + w.sum(axis=1, keepdims=True)
            total = total + jnp.dot(
                w.astype(jnp.bfloat16), rows(1, slot, cols), preferred_element_type=jnp.float32
            )
        out_ref[0, :, head * head_size:(head + 1) * head_size] = (total / weight_sum).astype(out_ref.dtype)


def attend(positions, live_counts, bias, queries, own_tiles, far_tiles, heads, head_size):
    _, token_count, width = queries.shape
    tile_count = token_count // TILE

    def whole(array):
        return pl.BlockSpec(array.shape, lambda t, pos, cnt: (0,) * array.ndim)

    kernel = functools.partial(
        attention_kernel, heads=heads, head_size=head_size, scale=1.0 / math.sqrt(head_size)
    )
    return pl.pallas_call(
        kernel,
        out_shape=jax.ShapeDtypeStruct((1, token_count, width), jnp.bfloat16),
        grid_spec=pltpu.PrefetchScalarGridSpec(
            num_scalar_prefetch=2,
            grid=(tile_count,),
            in_specs=[pl.BlockSpec(memory_space=pltpu.SMEM),
                      pl.BlockSpec((1, TILE, width), lambda t, pos, cnt: (0, t, 0)),
                      whole(own_tiles), whole(far_tiles)],
            out_specs=pl.BlockSpec((1, TILE, width), lambda t, pos, cnt: (0, t, 0)),
        ),
    )(positions, live_counts, bias, queries, own_tiles, far_tiles)


def partner_pairs(count, step):
    return [(source, source ^ step) for source in range(count)]


def local(clip_tokens, qkv_weight, out_weight, neighbours, counts, bias_index, rel_bias):
    heads_here = rel_bias.shape[0]
    width_here = out_weight.shape[0]
    head_size = width_here // heads_here
    token_count = clip_tokens.shape[1]
    tile_count = token_count // TILE
    n_ctx = lax.axis_size("ctx")
    n_dp = lax.axis_size("dp")
    own_index = lax.axis_index("ctx").astype(jnp.int32)
    devices = jnp.arange(n_ctx, dtype=jnp.int32)

    table = jnp.concatenate([neighbours, counts[:, None]], axis=1).astype(jnp.float32)
    all_table = lax.all_gather(table, "ctx", axis=0, tiled=True).astype(jnp.int32)
    all_table = all_table.reshape(n_ctx, tile_count, KMAX + 1)
    all_live = jnp.arange(KMAX)[None, None, :] < all_table[:, :, KMAX:]
    send_first, send_second = first_two(
        all_table[:, :, :KMAX], all_live, jnp.full((n_ctx,), own_index), tile_count
    )
    send_picks = jnp.stack([send_first, send_second], axis=1).reshape(-1)

    live = jnp.arange(KMAX)[None, :] < counts[:, None]
    recv_first, _ = first_two(
        jnp.broadcast_to(neighbours[None], (n_ctx,) + neighbours.shape),
        jnp.broadcast_to(live[None], (n_ctx,) + live.shape),
        devices,
        tile_count,
    )
    source = neighbours // tile_count
    within = neighbours % tile_count
    remote_slot = tile_count + CAP * source + jnp.where(within == recv_first[source], 0, 1)
    positions = jnp.where(source == own_index, within, remote_slot).astype(jnp.int32)
    bias = jnp.transpose(jnp.take(rel_bias, bias_index, axis=1), (1, 0, 2))
    live_counts = counts.astype(jnp.int32)

    own_tokens = clip_tokens[0]
    order = [3, 1, 2, 0] if n_dp == 4 else list(range(1, n_dp)) + [0]
    arrived = {0: own_tokens}
    for step in range(1, n_dp):
        arrived[step] = lax.ppermute(own_tokens, "dp", partner_pairs(n_dp, step))
    total = None
    received = []
    partials = []
    sent = []
    for index, step in enumerate(order):
        tokens = arrived[step]
        if index >= 1:
            tokens, _ = lax.optimization_barrier((tokens, received[max(index - 2, 0)]))
        projected = jnp.einsum(
            "td,sdh->sth", tokens, qkv_weight, preferred_element_type=jnp.float32
        ).astype(jnp.bfloat16)
        by_tile = jnp.transpose(
            projected[1:3].reshape(2, tile_count, TILE, width_here), (1, 0, 2, 3)
        )[:, :, None]
        payload = by_tile.at[send_picks].get(mode="promise_in_bounds")
        if index >= 2:
            payload, _ = lax.optimization_barrier((payload, partials[index - 2]))
        if index == len(order) - 1 and len(sent) >= 2:
            payload, _ = lax.optimization_barrier((payload, sent[-3]))
        incoming = lax.all_to_all(payload, "ctx", 0, 0, tiled=True)
        received.append(incoming)
        if index == len(order) - 1 and len(sent) >= 2:
            incoming, _ = lax.optimization_barrier((incoming, sent[-2]))
        attended = attend(positions, live_counts, bias, projected, by_tile, incoming, heads_here, head_size)
        partial_out = jnp.dot(
            attended[0], out_weight, preferred_element_type=jnp.float32
        ).astype(jnp.bfloat16)
        partials.append(partial_out)
        if step > 0:
            partial_out = lax.ppermute(partial_out, "dp", partner_pairs(n_dp, step))
            sent.append(partial_out)
        contribution = partial_out.astype(jnp.float32)
        total = contribution if total is None else total + contribution
    return total.astype(jnp.bfloat16)[None]


def solution(mesh):
    placed = (
        P("dp", "ctx", None),
        P(None, None, "dp"),
        P("dp", None),
        P("ctx", None),
        P("ctx"),
        P("ctx", None),
        P("dp", None),
    )
    return jax.shard_map(
        local, mesh=mesh, in_specs=placed, out_specs=P("dp", "ctx", None), check_vma=False
    )
```

```python
import functools
import math

import jax
import jax.numpy as jnp
from jax import lax
from jax.experimental import pallas as pl
from jax.experimental.pallas import tpu as pltpu
from jax.sharding import PartitionSpec as P

TILE = 64
REACH = 6
KMAX = 10
CAP = 2


def first_two(rows, rows_live, sources, tiles_per_device):
    local = jnp.arange(tiles_per_device, dtype=jnp.int32)
    wanted = sources[:, None] * tiles_per_device + local[None, :]
    named = jnp.any(
        (rows[:, :, :, None] == wanted[:, None, None, :]) & rows_live[:, :, :, None], axis=(1, 2)
    )
    order = jnp.where(named, local[None, :], tiles_per_device)
    first = jnp.min(order, axis=1)
    second = jnp.min(jnp.where(order > first[:, None], order, tiles_per_device), axis=1)
    first = jnp.where(first == tiles_per_device, 0, first)
    second = jnp.where(second == tiles_per_device, 0, second)
    return first.astype(jnp.int32), second.astype(jnp.int32)


def attention_kernel(pos_ref, count_ref, bias_ref, q_ref, own_ref, far_ref, out_ref, *, heads, head_size, scale):
    tile = pl.program_id(0)
    own_tiles = own_ref.shape[0]
    live_count = count_ref[tile]
    queries = q_ref[0]
    picks = []
    for slot in range(KMAX):
        where = pos_ref[tile, slot]
        picks.append((
            where < own_tiles,
            jnp.minimum(where, own_tiles - 1),
            jnp.maximum(where - own_tiles, 0),
        ))

    def rows(part, slot, cols):
        mine, near, far = picks[slot]
        return jnp.where(mine, own_ref[near, part, 0, :, cols], far_ref[far, part, 0, :, cols])

    for head in range(heads):
        cols = pl.ds(head * head_size, head_size)
        q_head = queries[:, head * head_size:(head + 1) * head_size]
        scores = []
        for slot in range(KMAX):
            s = lax.dot_general(
                q_head, rows(0, slot, cols), (((1,), (1,)), ((), ())),
                preferred_element_type=jnp.float32,
            )
            s = s * scale + bias_ref[tile, head, slot]
            s = jnp.where(slot < live_count, s, -1e30)
            scores.append(s)
        row_max = scores[0].max(axis=1, keepdims=True)
        for s in scores[1:]:
            row_max = jnp.maximum(row_max, s.max(axis=1, keepdims=True))
        total = jnp.zeros((TILE, head_size), jnp.float32)
        weight_sum = jnp.zeros((TILE, 1), jnp.float32)
        for slot in range(KMAX):
            w = jnp.exp(scores[slot] - row_max)
            weight_sum = weight_sum + w.sum(axis=1, keepdims=True)
            total = total + jnp.dot(
                w.astype(jnp.bfloat16), rows(1, slot, cols), preferred_element_type=jnp.float32
            )
        out_ref[0, :, head * head_size:(head + 1) * head_size] = (total / weight_sum).astype(out_ref.dtype)


def attend(positions, live_counts, bias, queries, own_tiles, far_tiles, heads, head_size):
    _, token_count, width = queries.shape
    tile_count = token_count // TILE

    def whole(array):
        return pl.BlockSpec(array.shape, lambda t, pos, cnt: (0,) * array.ndim)

    kernel = functools.partial(
        attention_kernel, heads=heads, head_size=head_size, scale=1.0 / math.sqrt(head_size)
    )
    return pl.pallas_call(
        kernel,
        out_shape=jax.ShapeDtypeStruct((1, token_count, width), jnp.bfloat16),
        grid_spec=pltpu.PrefetchScalarGridSpec(
            num_scalar_prefetch=2,
            grid=(tile_count,),
            in_specs=[pl.BlockSpec(memory_space=pltpu.SMEM),
                      pl.BlockSpec((1, TILE, width), lambda t, pos, cnt: (0, t, 0)),
                      whole(own_tiles), whole(far_tiles)],
            out_specs=pl.BlockSpec((1, TILE, width), lambda t, pos, cnt: (0, t, 0)),
        ),
    )(positions, live_counts, bias, queries, own_tiles, far_tiles)


def partner_pairs(count, step):
    return [(source, source ^ step) for source in range(count)]


def local(clip_tokens, qkv_weight, out_weight, neighbours, counts, bias_index, rel_bias):
    heads_here = rel_bias.shape[0]
    width_here = out_weight.shape[0]
    head_size = width_here // heads_here
    token_count = clip_tokens.shape[1]
    tile_count = token_count // TILE
    n_ctx = lax.axis_size("ctx")
    n_dp = lax.axis_size("dp")
    own_index = lax.axis_index("ctx").astype(jnp.int32)
    devices = jnp.arange(n_ctx, dtype=jnp.int32)

    table = jnp.concatenate([neighbours, counts[:, None]], axis=1).astype(jnp.float32)
    all_table = lax.all_gather(table, "ctx", axis=0, tiled=True).astype(jnp.int32)
    all_table = all_table.reshape(n_ctx, tile_count, KMAX + 1)
    all_live = jnp.arange(KMAX)[None, None, :] < all_table[:, :, KMAX:]
    send_first, send_second = first_two(
        all_table[:, :, :KMAX], all_live, jnp.full((n_ctx,), own_index), tile_count
    )
    send_picks = jnp.stack([send_first, send_second], axis=1).reshape(-1)

    live = jnp.arange(KMAX)[None, :] < counts[:, None]
    recv_first, _ = first_two(
        jnp.broadcast_to(neighbours[None], (n_ctx,) + neighbours.shape),
        jnp.broadcast_to(live[None], (n_ctx,) + live.shape),
        devices,
        tile_count,
    )
    source = neighbours // tile_count
    within = neighbours % tile_count
    remote_slot = tile_count + CAP * source + jnp.where(within == recv_first[source], 0, 1)
    positions = jnp.where(source == own_index, within, remote_slot).astype(jnp.int32)
    bias = jnp.transpose(jnp.take(rel_bias, bias_index, axis=1), (1, 0, 2))
    live_counts = counts.astype(jnp.int32)

    own_tokens = clip_tokens[0]
    order = [0, 3, 2, 1] if n_dp == 4 else list(range(n_dp))
    arrived = {0: own_tokens}
    for step in range(1, n_dp):
        arrived[step] = lax.ppermute(own_tokens, "dp", partner_pairs(n_dp, step))
    last = order[-1]
    total = None
    received = []
    partials = []
    sent = []
    far_weight = None
    for index, step in enumerate(order):
        final = index == len(order) - 1
        tokens = arrived[step]
        if index >= 1:
            tokens, _ = lax.optimization_barrier((tokens, received[max(index - 2, 0)]))
        if index == 1 and last > 0:
            held, _ = lax.optimization_barrier((out_weight, received[0]))
            far_weight = lax.ppermute(held, "dp", partner_pairs(n_dp, last))
        projected = jnp.einsum(
            "td,sdh->sth", tokens, qkv_weight, preferred_element_type=jnp.float32
        ).astype(jnp.bfloat16)
        by_tile = jnp.transpose(
            projected[1:3].reshape(2, tile_count, TILE, width_here), (1, 0, 2, 3)
        )[:, :, None]
        payload = by_tile.at[send_picks].get(mode="promise_in_bounds")
        if index >= 2:
            payload, _ = lax.optimization_barrier((payload, partials[index - 2]))
        if final and len(sent) >= 2:
            payload, _ = lax.optimization_barrier((payload, sent[-2]))
        incoming = lax.all_to_all(payload, "ctx", 0, 0, tiled=True)
        received.append(incoming)
        attended = attend(positions, live_counts, bias, projected, by_tile, incoming, heads_here, head_size)
        if final and step > 0:
            came = lax.ppermute(attended[0], "dp", partner_pairs(n_dp, step))
            weight = far_weight if far_weight is not None else lax.ppermute(
                out_weight, "dp", partner_pairs(n_dp, step)
            )
            partial_out = jnp.dot(came, weight, preferred_element_type=jnp.float32).astype(jnp.bfloat16)
        else:
            partial_out = jnp.dot(
                attended[0], out_weight, preferred_element_type=jnp.float32
            ).astype(jnp.bfloat16)
            partials.append(partial_out)
            if step > 0:
                partial_out = lax.ppermute(partial_out, "dp", partner_pairs(n_dp, step))
                sent.append(partial_out)
        contribution = partial_out.astype(jnp.float32)
        total = contribution if total is None else total + contribution
    return total.astype(jnp.bfloat16)[None]


def solution(mesh):
    placed = (
        P("dp", "ctx", None),
        P(None, None, "dp"),
        P("dp", None),
        P("ctx", None),
        P("ctx"),
        P("ctx", None),
        P("dp", None),
    )
    return jax.shard_map(
        local, mesh=mesh, in_specs=placed, out_specs=P("dp", "ctx", None), check_vma=False
    )
```

```python
import functools
import math

import jax
import jax.numpy as jnp
from jax import lax
from jax.experimental import pallas as pl
from jax.experimental.pallas import tpu as pltpu
from jax.sharding import PartitionSpec as P

TILE = 64
REACH = 6
KMAX = 10
CAP = 2


def first_two(rows, rows_live, sources, tiles_per_device):
    local = jnp.arange(tiles_per_device, dtype=jnp.int32)
    wanted = sources[:, None] * tiles_per_device + local[None, :]
    named = jnp.any(
        (rows[:, :, :, None] == wanted[:, None, None, :]) & rows_live[:, :, :, None], axis=(1, 2)
    )
    order = jnp.where(named, local[None, :], tiles_per_device)
    first = jnp.min(order, axis=1)
    second = jnp.min(jnp.where(order > first[:, None], order, tiles_per_device), axis=1)
    first = jnp.where(first == tiles_per_device, 0, first)
    second = jnp.where(second == tiles_per_device, 0, second)
    return first.astype(jnp.int32), second.astype(jnp.int32)


def attention_kernel(pos_ref, count_ref, bias_ref, q_ref, own_ref, far_ref, out_ref, *, heads, head_size, scale):
    tile = pl.program_id(0)
    own_tiles = own_ref.shape[0]
    live_count = count_ref[tile]
    queries = q_ref[0]
    picks = []
    for slot in range(KMAX):
        where = pos_ref[tile, slot]
        picks.append((
            where < own_tiles,
            jnp.minimum(where, own_tiles - 1),
            jnp.maximum(where - own_tiles, 0),
        ))

    def rows(part, slot, cols):
        mine, near, far = picks[slot]
        return jnp.where(mine, own_ref[near, part, 0, :, cols], far_ref[far, part, 0, :, cols])

    column = lax.broadcasted_iota(jnp.int32, (1, KMAX * TILE), 1) // TILE
    live = column < live_count
    for head in range(heads):
        cols = pl.ds(head * head_size, head_size)
        q_head = queries[:, head * head_size:(head + 1) * head_size]
        keys = jnp.concatenate([rows(0, slot, cols) for slot in range(KMAX)], axis=0)
        values = jnp.concatenate([rows(1, slot, cols) for slot in range(KMAX)], axis=0)
        bias_row = jnp.zeros((1, KMAX * TILE), jnp.float32)
        for slot in range(KMAX):
            bias_row = jnp.where(column == slot, bias_ref[tile, head, slot], bias_row)
        s = lax.dot_general(
            q_head, keys, (((1,), (1,)), ((), ())), preferred_element_type=jnp.float32
        )
        s = jnp.where(live, s * scale + bias_row, -1e30)
        row_max = s.max(axis=1, keepdims=True)
        w = jnp.exp(s - row_max)
        weight_sum = w.sum(axis=1, keepdims=True)
        total = jnp.dot(w.astype(jnp.bfloat16), values, preferred_element_type=jnp.float32)
        out_ref[0, :, head * head_size:(head + 1) * head_size] = (total / weight_sum).astype(out_ref.dtype)


def attend(positions, live_counts, bias, queries, own_tiles, far_tiles, heads, head_size):
    _, token_count, width = queries.shape
    tile_count = token_count // TILE

    def whole(array):
        return pl.BlockSpec(array.shape, lambda t, pos, cnt: (0,) * array.ndim)

    kernel = functools.partial(
        attention_kernel, heads=heads, head_size=head_size, scale=1.0 / math.sqrt(head_size)
    )
    return pl.pallas_call(
        kernel,
        out_shape=jax.ShapeDtypeStruct((1, token_count, width), jnp.bfloat16),
        grid_spec=pltpu.PrefetchScalarGridSpec(
            num_scalar_prefetch=2,
            grid=(tile_count,),
            in_specs=[pl.BlockSpec(memory_space=pltpu.SMEM),
                      pl.BlockSpec((1, TILE, width), lambda t, pos, cnt: (0, t, 0)),
                      whole(own_tiles), whole(far_tiles)],
            out_specs=pl.BlockSpec((1, TILE, width), lambda t, pos, cnt: (0, t, 0)),
        ),
    )(positions, live_counts, bias, queries, own_tiles, far_tiles)


def partner_pairs(count, step):
    return [(source, source ^ step) for source in range(count)]


def local(clip_tokens, qkv_weight, out_weight, neighbours, counts, bias_index, rel_bias):
    heads_here = rel_bias.shape[0]
    width_here = out_weight.shape[0]
    head_size = width_here // heads_here
    token_count = clip_tokens.shape[1]
    tile_count = token_count // TILE
    n_ctx = lax.axis_size("ctx")
    n_dp = lax.axis_size("dp")
    own_index = lax.axis_index("ctx").astype(jnp.int32)
    devices = jnp.arange(n_ctx, dtype=jnp.int32)

    table = jnp.concatenate([neighbours, counts[:, None]], axis=1).astype(jnp.float32)
    all_table = lax.all_gather(table, "ctx", axis=0, tiled=True).astype(jnp.int32)
    all_table = all_table.reshape(n_ctx, tile_count, KMAX + 1)
    all_live = jnp.arange(KMAX)[None, None, :] < all_table[:, :, KMAX:]
    send_first, send_second = first_two(
        all_table[:, :, :KMAX], all_live, jnp.full((n_ctx,), own_index), tile_count
    )
    send_picks = jnp.stack([send_first, send_second], axis=1).reshape(-1)

    live = jnp.arange(KMAX)[None, :] < counts[:, None]
    recv_first, _ = first_two(
        jnp.broadcast_to(neighbours[None], (n_ctx,) + neighbours.shape),
        jnp.broadcast_to(live[None], (n_ctx,) + live.shape),
        devices,
        tile_count,
    )
    source = neighbours // tile_count
    within = neighbours % tile_count
    remote_slot = tile_count + CAP * source + jnp.where(within == recv_first[source], 0, 1)
    positions = jnp.where(source == own_index, within, remote_slot).astype(jnp.int32)
    bias = jnp.transpose(jnp.take(rel_bias, bias_index, axis=1), (1, 0, 2))
    live_counts = counts.astype(jnp.int32)

    own_tokens = clip_tokens[0]
    order = [3, 1, 2, 0] if n_dp == 4 else list(range(1, n_dp)) + [0]
    arrived = {0: own_tokens}
    for step in range(1, n_dp):
        arrived[step] = lax.ppermute(own_tokens, "dp", partner_pairs(n_dp, step))
    total = None
    received = []
    partials = []
    sent = []
    for index, step in enumerate(order):
        tokens = arrived[step]
        if index >= 1:
            tokens, _ = lax.optimization_barrier((tokens, received[max(index - 2, 0)]))
        projected = jnp.einsum(
            "td,sdh->sth", tokens, qkv_weight, preferred_element_type=jnp.float32
        ).astype(jnp.bfloat16)
        by_tile = jnp.transpose(
            projected[1:3].reshape(2, tile_count, TILE, width_here), (1, 0, 2, 3)
        )[:, :, None]
        payload = by_tile.at[send_picks].get(mode="promise_in_bounds")
        if index >= 2:
            payload, _ = lax.optimization_barrier((payload, partials[index - 2]))
        if index == len(order) - 1 and len(sent) >= 2:
            payload, _ = lax.optimization_barrier((payload, sent[-3]))
        incoming = lax.all_to_all(payload, "ctx", 0, 0, tiled=True)
        received.append(incoming)
        if index == len(order) - 1 and len(sent) >= 2:
            incoming, _ = lax.optimization_barrier((incoming, sent[-2]))
        attended = attend(positions, live_counts, bias, projected, by_tile, incoming, heads_here, head_size)
        partial_out = jnp.dot(
            attended[0], out_weight, preferred_element_type=jnp.float32
        ).astype(jnp.bfloat16)
        partials.append(partial_out)
        if step > 0:
            partial_out = lax.ppermute(partial_out, "dp", partner_pairs(n_dp, step))
            sent.append(partial_out)
        contribution = partial_out.astype(jnp.float32)
        total = contribution if total is None else total + contribution
    return total.astype(jnp.bfloat16)[None]


def solution(mesh):
    placed = (
        P("dp", "ctx", None),
        P(None, None, "dp"),
        P("dp", None),
        P("ctx", None),
        P("ctx"),
        P("ctx", None),
        P("dp", None),
    )
    return jax.shard_map(
        local, mesh=mesh, in_specs=placed, out_specs=P("dp", "ctx", None), check_vma=False
    )
```

```python
import functools
import math

import jax
import jax.numpy as jnp
from jax import lax
from jax.experimental import pallas as pl
from jax.experimental.pallas import tpu as pltpu
from jax.sharding import PartitionSpec as P

TILE = 64
REACH = 6
KMAX = 10
CAP = 2


def first_two(rows, rows_live, sources, tiles_per_device):
    local = jnp.arange(tiles_per_device, dtype=jnp.int32)
    wanted = sources[:, None] * tiles_per_device + local[None, :]
    named = jnp.any(
        (rows[:, :, :, None] == wanted[:, None, None, :]) & rows_live[:, :, :, None], axis=(1, 2)
    )
    order = jnp.where(named, local[None, :], tiles_per_device)
    first = jnp.min(order, axis=1)
    second = jnp.min(jnp.where(order > first[:, None], order, tiles_per_device), axis=1)
    first = jnp.where(first == tiles_per_device, 0, first)
    second = jnp.where(second == tiles_per_device, 0, second)
    return first.astype(jnp.int32), second.astype(jnp.int32)


def attention_kernel(pos_ref, count_ref, bias_ref, q_ref, own_ref, far_ref, out_ref, *, heads, head_size, scale):
    tile = pl.program_id(0)
    own_tiles = own_ref.shape[0]
    live_count = count_ref[tile]
    queries = q_ref[0]
    picks = []
    for slot in range(KMAX):
        where = pos_ref[tile, slot]
        picks.append((
            where < own_tiles,
            jnp.minimum(where, own_tiles - 1),
            jnp.maximum(where - own_tiles, 0),
        ))

    def rows(part, slot, cols):
        mine, near, far = picks[slot]
        return jnp.where(mine, own_ref[near, part, 0, :, cols], far_ref[far, part, 0, :, cols])

    column = lax.broadcasted_iota(jnp.int32, (1, KMAX * TILE), 1) // TILE
    live = column < live_count
    for head in range(heads):
        cols = pl.ds(head * head_size, head_size)
        q_head = queries[:, head * head_size:(head + 1) * head_size]
        keys = jnp.concatenate([rows(0, slot, cols) for slot in range(KMAX)], axis=0)
        values = jnp.concatenate([rows(1, slot, cols) for slot in range(KMAX)], axis=0)
        bias_row = jnp.zeros((1, KMAX * TILE), jnp.float32)
        for slot in range(KMAX):
            bias_row = jnp.where(column == slot, bias_ref[tile, head, slot], bias_row)
        s = lax.dot_general(
            q_head, keys, (((1,), (1,)), ((), ())), preferred_element_type=jnp.float32
        )
        s = jnp.where(live, s * scale + bias_row, -1e30)
        row_max = s.max(axis=1, keepdims=True)
        w = jnp.exp(s - row_max)
        weight_sum = w.sum(axis=1, keepdims=True)
        total = jnp.dot(w.astype(jnp.bfloat16), values, preferred_element_type=jnp.float32)
        out_ref[0, :, head * head_size:(head + 1) * head_size] = (total / weight_sum).astype(out_ref.dtype)


def attend(positions, live_counts, bias, queries, own_tiles, far_tiles, heads, head_size):
    _, token_count, width = queries.shape
    tile_count = token_count // TILE

    def whole(array):
        return pl.BlockSpec(array.shape, lambda t, pos, cnt: (0,) * array.ndim)

    kernel = functools.partial(
        attention_kernel, heads=heads, head_size=head_size, scale=1.0 / math.sqrt(head_size)
    )
    return pl.pallas_call(
        kernel,
        out_shape=jax.ShapeDtypeStruct((1, token_count, width), jnp.bfloat16),
        grid_spec=pltpu.PrefetchScalarGridSpec(
            num_scalar_prefetch=2,
            grid=(tile_count,),
            in_specs=[pl.BlockSpec(memory_space=pltpu.SMEM),
                      pl.BlockSpec((1, TILE, width), lambda t, pos, cnt: (0, t, 0)),
                      whole(own_tiles), whole(far_tiles)],
            out_specs=pl.BlockSpec((1, TILE, width), lambda t, pos, cnt: (0, t, 0)),
        ),
    )(positions, live_counts, bias, queries, own_tiles, far_tiles)


def partner_pairs(count, step):
    return [(source, source ^ step) for source in range(count)]


def local(clip_tokens, qkv_weight, out_weight, neighbours, counts, bias_index, rel_bias):
    heads_here = rel_bias.shape[0]
    width_here = out_weight.shape[0]
    head_size = width_here // heads_here
    token_count = clip_tokens.shape[1]
    tile_count = token_count // TILE
    n_ctx = lax.axis_size("ctx")
    n_dp = lax.axis_size("dp")
    own_index = lax.axis_index("ctx").astype(jnp.int32)
    devices = jnp.arange(n_ctx, dtype=jnp.int32)

    table = jnp.concatenate([neighbours, counts[:, None]], axis=1).astype(jnp.float32)
    all_table = lax.all_gather(table, "ctx", axis=0, tiled=True).astype(jnp.int32)
    all_table = all_table.reshape(n_ctx, tile_count, KMAX + 1)
    all_live = jnp.arange(KMAX)[None, None, :] < all_table[:, :, KMAX:]
    send_first, send_second = first_two(
        all_table[:, :, :KMAX], all_live, jnp.full((n_ctx,), own_index), tile_count
    )
    send_picks = jnp.stack([send_first, send_second], axis=1).reshape(-1)

    live = jnp.arange(KMAX)[None, :] < counts[:, None]
    recv_first, _ = first_two(
        jnp.broadcast_to(neighbours[None], (n_ctx,) + neighbours.shape),
        jnp.broadcast_to(live[None], (n_ctx,) + live.shape),
        devices,
        tile_count,
    )
    source = neighbours // tile_count
    within = neighbours % tile_count
    remote_slot = tile_count + CAP * source + jnp.where(within == recv_first[source], 0, 1)
    positions = jnp.where(source == own_index, within, remote_slot).astype(jnp.int32)
    bias = jnp.transpose(jnp.take(rel_bias, bias_index, axis=1), (1, 0, 2))
    live_counts = counts.astype(jnp.int32)

    own_tokens = clip_tokens[0]
    order = [3, 1, 2, 0] if n_dp == 4 else list(range(1, n_dp)) + [0]
    arrived = {0: own_tokens}
    for step in range(1, n_dp):
        arrived[step] = lax.ppermute(own_tokens, "dp", partner_pairs(n_dp, step))
    total = None
    received = []
    partials = []
    sent = []
    for index, step in enumerate(order):
        tokens = arrived[step]
        if index >= 1:
            tokens, _ = lax.optimization_barrier((tokens, received[max(index - 2, 0)]))
        key_value = jnp.einsum(
            "td,sdh->sth", tokens, qkv_weight[1:3], preferred_element_type=jnp.float32
        ).astype(jnp.bfloat16)
        by_tile = jnp.transpose(
            key_value.reshape(2, tile_count, TILE, width_here), (1, 0, 2, 3)
        )[:, :, None]
        payload = by_tile.at[send_picks].get(mode="promise_in_bounds")
        if index >= 2:
            payload, _ = lax.optimization_barrier((payload, partials[index - 2]))
        if index == len(order) - 1 and len(sent) >= 2:
            payload, _ = lax.optimization_barrier((payload, sent[-3]))
        incoming = lax.all_to_all(payload, "ctx", 0, 0, tiled=True)
        received.append(incoming)
        if index == len(order) - 1 and len(sent) >= 2:
            incoming, _ = lax.optimization_barrier((incoming, sent[-2]))
        queries = jnp.dot(tokens, qkv_weight[0], preferred_element_type=jnp.float32).astype(jnp.bfloat16)
        attended = attend(positions, live_counts, bias, queries[None], by_tile, incoming, heads_here, head_size)
        partial_out = jnp.dot(
            attended[0], out_weight, preferred_element_type=jnp.float32
        ).astype(jnp.bfloat16)
        partials.append(partial_out)
        if step > 0:
            partial_out = lax.ppermute(partial_out, "dp", partner_pairs(n_dp, step))
            sent.append(partial_out)
        contribution = partial_out.astype(jnp.float32)
        total = contribution if total is None else total + contribution
    return total.astype(jnp.bfloat16)[None]


def solution(mesh):
    placed = (
        P("dp", "ctx", None),
        P(None, None, "dp"),
        P("dp", None),
        P("ctx", None),
        P("ctx"),
        P("ctx", None),
        P("dp", None),
    )
    return jax.shard_map(
        local, mesh=mesh, in_specs=placed, out_specs=P("dp", "ctx", None), check_vma=False
    )
```

```python
import functools
import math

import jax
import jax.numpy as jnp
from jax import lax
from jax.experimental import pallas as pl
from jax.experimental.pallas import tpu as pltpu
from jax.sharding import PartitionSpec as P

TILE = 64
REACH = 6
KMAX = 10
CAP = 2


def first_two(rows, rows_live, sources, tiles_per_device):
    local = jnp.arange(tiles_per_device, dtype=jnp.int32)
    wanted = sources[:, None] * tiles_per_device + local[None, :]
    named = jnp.any(
        (rows[:, :, :, None] == wanted[:, None, None, :]) & rows_live[:, :, :, None], axis=(1, 2)
    )
    order = jnp.where(named, local[None, :], tiles_per_device)
    first = jnp.min(order, axis=1)
    second = jnp.min(jnp.where(order > first[:, None], order, tiles_per_device), axis=1)
    first = jnp.where(first == tiles_per_device, 0, first)
    second = jnp.where(second == tiles_per_device, 0, second)
    return first.astype(jnp.int32), second.astype(jnp.int32)


def attention_kernel(pos_ref, count_ref, bias_ref, q_ref, own_ref, far_ref, out_ref, *, heads, head_size, scale):
    tile = pl.program_id(0)
    own_tiles = own_ref.shape[0]
    live_count = count_ref[tile]
    queries = q_ref[0]
    picks = []
    for slot in range(KMAX):
        where = pos_ref[tile, slot]
        picks.append((
            where < own_tiles,
            jnp.minimum(where, own_tiles - 1),
            jnp.maximum(where - own_tiles, 0),
        ))

    def rows(part, slot, cols):
        mine, near, far = picks[slot]
        return jnp.where(mine, own_ref[near, part, 0, :, cols], far_ref[far, part, 0, :, cols])

    column = lax.broadcasted_iota(jnp.int32, (1, KMAX * TILE), 1) // TILE
    live = column < live_count
    for head in range(heads):
        cols = pl.ds(head * head_size, head_size)
        q_head = queries[:, head * head_size:(head + 1) * head_size]
        keys = jnp.concatenate([rows(0, slot, cols) for slot in range(KMAX)], axis=0)
        values = jnp.concatenate([rows(1, slot, cols) for slot in range(KMAX)], axis=0)
        bias_row = jnp.zeros((1, KMAX * TILE), jnp.float32)
        for slot in range(KMAX):
            bias_row = jnp.where(column == slot, bias_ref[tile, head, slot], bias_row)
        s = lax.dot_general(
            q_head, keys, (((1,), (1,)), ((), ())), preferred_element_type=jnp.float32
        )
        s = jnp.where(live, s * scale + bias_row, -1e30)
        row_max = s.max(axis=1, keepdims=True)
        w = jnp.exp(s - row_max)
        weight_sum = w.sum(axis=1, keepdims=True)
        total = jnp.dot(w.astype(jnp.bfloat16), values, preferred_element_type=jnp.float32)
        out_ref[0, :, head * head_size:(head + 1) * head_size] = (total / weight_sum).astype(out_ref.dtype)


def attend(positions, live_counts, bias, queries, own_tiles, far_tiles, heads, head_size):
    _, token_count, width = queries.shape
    tile_count = token_count // TILE

    def whole(array):
        return pl.BlockSpec(array.shape, lambda t, pos, cnt: (0,) * array.ndim)

    kernel = functools.partial(
        attention_kernel, heads=heads, head_size=head_size, scale=1.0 / math.sqrt(head_size)
    )
    return pl.pallas_call(
        kernel,
        out_shape=jax.ShapeDtypeStruct((1, token_count, width), jnp.bfloat16),
        grid_spec=pltpu.PrefetchScalarGridSpec(
            num_scalar_prefetch=2,
            grid=(tile_count,),
            in_specs=[pl.BlockSpec(memory_space=pltpu.SMEM),
                      pl.BlockSpec((1, TILE, width), lambda t, pos, cnt: (0, t, 0)),
                      whole(own_tiles), whole(far_tiles)],
            out_specs=pl.BlockSpec((1, TILE, width), lambda t, pos, cnt: (0, t, 0)),
        ),
    )(positions, live_counts, bias, queries, own_tiles, far_tiles)


def partner_pairs(count, step):
    return [(source, source ^ step) for source in range(count)]


def local(clip_tokens, qkv_weight, out_weight, neighbours, counts, bias_index, rel_bias):
    heads_here = rel_bias.shape[0]
    width_here = out_weight.shape[0]
    head_size = width_here // heads_here
    token_count = clip_tokens.shape[1]
    tile_count = token_count // TILE
    n_ctx = lax.axis_size("ctx")
    n_dp = lax.axis_size("dp")
    own_index = lax.axis_index("ctx").astype(jnp.int32)
    devices = jnp.arange(n_ctx, dtype=jnp.int32)

    table = jnp.concatenate([neighbours, counts[:, None]], axis=1).astype(jnp.float32)
    all_table = lax.all_gather(table, "ctx", axis=0, tiled=True).astype(jnp.int32)
    all_table = all_table.reshape(n_ctx, tile_count, KMAX + 1)
    all_live = jnp.arange(KMAX)[None, None, :] < all_table[:, :, KMAX:]
    send_first, send_second = first_two(
        all_table[:, :, :KMAX], all_live, jnp.full((n_ctx,), own_index), tile_count
    )
    send_picks = jnp.stack([send_first, send_second], axis=1).reshape(-1)

    live = jnp.arange(KMAX)[None, :] < counts[:, None]
    recv_first, _ = first_two(
        jnp.broadcast_to(neighbours[None], (n_ctx,) + neighbours.shape),
        jnp.broadcast_to(live[None], (n_ctx,) + live.shape),
        devices,
        tile_count,
    )
    source = neighbours // tile_count
    within = neighbours % tile_count
    remote_slot = tile_count + CAP * source + jnp.where(within == recv_first[source], 0, 1)
    positions = jnp.where(source == own_index, within, remote_slot).astype(jnp.int32)
    bias = jnp.transpose(jnp.take(rel_bias, bias_index, axis=1), (1, 0, 2))
    live_counts = counts.astype(jnp.int32)

    own_tokens = clip_tokens[0]
    order = [3, 1, 2, 0] if n_dp == 4 else list(range(1, n_dp)) + [0]
    arrived = {0: own_tokens}
    for step in range(1, n_dp):
        arrived[step] = lax.ppermute(own_tokens, "dp", partner_pairs(n_dp, step))
    total = None
    received = []
    partials = []
    sent = []
    for index, step in enumerate(order):
        tokens = arrived[step]
        if index >= 2:
            tokens, _ = lax.optimization_barrier((tokens, received[index - 2]))
        projected = jnp.einsum(
            "td,sdh->sth", tokens, qkv_weight, preferred_element_type=jnp.float32
        ).astype(jnp.bfloat16)
        by_tile = jnp.transpose(
            projected[1:3].reshape(2, tile_count, TILE, width_here), (1, 0, 2, 3)
        )[:, :, None]
        payload = by_tile.at[send_picks].get(mode="promise_in_bounds")
        if index >= 2:
            payload, _ = lax.optimization_barrier((payload, partials[index - 2]))
        if index == len(order) - 1 and len(sent) >= 2:
            payload, _ = lax.optimization_barrier((payload, sent[-3]))
        incoming = lax.all_to_all(payload, "ctx", 0, 0, tiled=True)
        received.append(incoming)
        if index == len(order) - 1 and len(sent) >= 2:
            incoming, _ = lax.optimization_barrier((incoming, sent[-2]))
        attended = attend(positions, live_counts, bias, projected, by_tile, incoming, heads_here, head_size)
        partial_out = jnp.dot(
            attended[0], out_weight, preferred_element_type=jnp.float32
        ).astype(jnp.bfloat16)
        partials.append(partial_out)
        if step > 0:
            partial_out = lax.ppermute(partial_out, "dp", partner_pairs(n_dp, step))
            sent.append(partial_out)
        contribution = partial_out.astype(jnp.float32)
        total = contribution if total is None else total + contribution
    return total.astype(jnp.bfloat16)[None]


def solution(mesh):
    placed = (
        P("dp", "ctx", None),
        P(None, None, "dp"),
        P("dp", None),
        P("ctx", None),
        P("ctx"),
        P("ctx", None),
        P("dp", None),
    )
    return jax.shard_map(
        local, mesh=mesh, in_specs=placed, out_specs=P("dp", "ctx", None), check_vma=False
    )
```

```python
import functools
import math

import jax
import jax.numpy as jnp
from jax import lax
from jax.experimental import pallas as pl
from jax.experimental.pallas import tpu as pltpu
from jax.sharding import PartitionSpec as P

TILE = 64
REACH = 6
KMAX = 10
CAP = 2


def first_two(rows, rows_live, sources, tiles_per_device):
    local = jnp.arange(tiles_per_device, dtype=jnp.int32)
    wanted = sources[:, None] * tiles_per_device + local[None, :]
    named = jnp.any(
        (rows[:, :, :, None] == wanted[:, None, None, :]) & rows_live[:, :, :, None], axis=(1, 2)
    )
    order = jnp.where(named, local[None, :], tiles_per_device)
    first = jnp.min(order, axis=1)
    second = jnp.min(jnp.where(order > first[:, None], order, tiles_per_device), axis=1)
    first = jnp.where(first == tiles_per_device, 0, first)
    second = jnp.where(second == tiles_per_device, 0, second)
    return first.astype(jnp.int32), second.astype(jnp.int32)


def attention_kernel(pos_ref, count_ref, bias_ref, q_ref, own_ref, far_ref, w_ref, out_ref, *, heads, head_size, scale):
    tile = pl.program_id(0)
    own_tiles = own_ref.shape[0]
    live_count = count_ref[tile]
    queries = q_ref[0]
    picks = []
    for slot in range(KMAX):
        where = pos_ref[tile, slot]
        picks.append((
            where < own_tiles,
            jnp.minimum(where, own_tiles - 1),
            jnp.maximum(where - own_tiles, 0),
        ))

    def rows(part, slot, cols):
        mine, near, far = picks[slot]
        return jnp.where(mine, own_ref[near, part, 0, :, cols], far_ref[far, part, 0, :, cols])

    column = lax.broadcasted_iota(jnp.int32, (1, KMAX * TILE), 1) // TILE
    live = column < live_count
    attended = []
    for head in range(heads):
        cols = pl.ds(head * head_size, head_size)
        q_head = queries[:, head * head_size:(head + 1) * head_size]
        keys = jnp.concatenate([rows(0, slot, cols) for slot in range(KMAX)], axis=0)
        values = jnp.concatenate([rows(1, slot, cols) for slot in range(KMAX)], axis=0)
        bias_row = jnp.zeros((1, KMAX * TILE), jnp.float32)
        for slot in range(KMAX):
            bias_row = jnp.where(column == slot, bias_ref[tile, head, slot], bias_row)
        s = lax.dot_general(
            q_head, keys, (((1,), (1,)), ((), ())), preferred_element_type=jnp.float32
        )
        s = jnp.where(live, s * scale + bias_row, -1e30)
        row_max = s.max(axis=1, keepdims=True)
        w = jnp.exp(s - row_max)
        weight_sum = w.sum(axis=1, keepdims=True)
        total = jnp.dot(w.astype(jnp.bfloat16), values, preferred_element_type=jnp.float32)
        attended.append((total / weight_sum).astype(jnp.bfloat16))
    merged = jnp.concatenate(attended, axis=1)
    out_ref[0] = jnp.dot(merged, w_ref[...], preferred_element_type=jnp.float32).astype(out_ref.dtype)


def attend(positions, live_counts, bias, queries, own_tiles, far_tiles, weight, heads, head_size):
    _, token_count, width = queries.shape
    out_width = weight.shape[1]
    tile_count = token_count // TILE

    def whole(array):
        return pl.BlockSpec(array.shape, lambda t, pos, cnt: (0,) * array.ndim)

    kernel = functools.partial(
        attention_kernel, heads=heads, head_size=head_size, scale=1.0 / math.sqrt(head_size)
    )
    return pl.pallas_call(
        kernel,
        out_shape=jax.ShapeDtypeStruct((1, token_count, out_width), jnp.bfloat16),
        grid_spec=pltpu.PrefetchScalarGridSpec(
            num_scalar_prefetch=2,
            grid=(tile_count,),
            in_specs=[pl.BlockSpec(memory_space=pltpu.SMEM),
                      pl.BlockSpec((1, TILE, width), lambda t, pos, cnt: (0, t, 0)),
                      whole(own_tiles), whole(far_tiles), whole(weight)],
            out_specs=pl.BlockSpec((1, TILE, out_width), lambda t, pos, cnt: (0, t, 0)),
        ),
    )(positions, live_counts, bias, queries, own_tiles, far_tiles, weight)


def partner_pairs(count, step):
    return [(source, source ^ step) for source in range(count)]


def local(clip_tokens, qkv_weight, out_weight, neighbours, counts, bias_index, rel_bias):
    heads_here = rel_bias.shape[0]
    width_here = out_weight.shape[0]
    head_size = width_here // heads_here
    token_count = clip_tokens.shape[1]
    tile_count = token_count // TILE
    n_ctx = lax.axis_size("ctx")
    n_dp = lax.axis_size("dp")
    own_index = lax.axis_index("ctx").astype(jnp.int32)
    devices = jnp.arange(n_ctx, dtype=jnp.int32)

    table = jnp.concatenate([neighbours, counts[:, None]], axis=1).astype(jnp.float32)
    all_table = lax.all_gather(table, "ctx", axis=0, tiled=True).astype(jnp.int32)
    all_table = all_table.reshape(n_ctx, tile_count, KMAX + 1)
    all_live = jnp.arange(KMAX)[None, None, :] < all_table[:, :, KMAX:]
    send_first, send_second = first_two(
        all_table[:, :, :KMAX], all_live, jnp.full((n_ctx,), own_index), tile_count
    )
    send_picks = jnp.stack([send_first, send_second], axis=1).reshape(-1)

    live = jnp.arange(KMAX)[None, :] < counts[:, None]
    recv_first, _ = first_two(
        jnp.broadcast_to(neighbours[None], (n_ctx,) + neighbours.shape),
        jnp.broadcast_to(live[None], (n_ctx,) + live.shape),
        devices,
        tile_count,
    )
    source = neighbours // tile_count
    within = neighbours % tile_count
    remote_slot = tile_count + CAP * source + jnp.where(within == recv_first[source], 0, 1)
    positions = jnp.where(source == own_index, within, remote_slot).astype(jnp.int32)
    bias = jnp.transpose(jnp.take(rel_bias, bias_index, axis=1), (1, 0, 2))
    live_counts = counts.astype(jnp.int32)

    own_tokens = clip_tokens[0]
    order = [3, 1, 2, 0] if n_dp == 4 else list(range(1, n_dp)) + [0]
    arrived = {0: own_tokens}
    for step in range(1, n_dp):
        arrived[step] = lax.ppermute(own_tokens, "dp", partner_pairs(n_dp, step))
    total = None
    received = []
    partials = []
    sent = []
    for index, step in enumerate(order):
        tokens = arrived[step]
        if index >= 2:
            tokens, _ = lax.optimization_barrier((tokens, received[index - 2]))
        projected = jnp.einsum(
            "td,sdh->sth", tokens, qkv_weight, preferred_element_type=jnp.float32
        ).astype(jnp.bfloat16)
        by_tile = jnp.transpose(
            projected[1:3].reshape(2, tile_count, TILE, width_here), (1, 0, 2, 3)
        )[:, :, None]
        payload = by_tile.at[send_picks].get(mode="promise_in_bounds")
        if index >= 2:
            payload, _ = lax.optimization_barrier((payload, partials[index - 2]))
        if index == len(order) - 1 and len(sent) >= 2:
            payload, _ = lax.optimization_barrier((payload, sent[-3]))
        incoming = lax.all_to_all(payload, "ctx", 0, 0, tiled=True)
        received.append(incoming)
        if index == len(order) - 1 and len(sent) >= 2:
            incoming, _ = lax.optimization_barrier((incoming, sent[-2]))
        partial_out = attend(
            positions, live_counts, bias, projected, by_tile, incoming, out_weight, heads_here, head_size
        )[0]
        partials.append(partial_out)
        if step > 0:
            partial_out = lax.ppermute(partial_out, "dp", partner_pairs(n_dp, step))
            sent.append(partial_out)
        contribution = partial_out.astype(jnp.float32)
        total = contribution if total is None else total + contribution
    return total.astype(jnp.bfloat16)[None]


def solution(mesh):
    placed = (
        P("dp", "ctx", None),
        P(None, None, "dp"),
        P("dp", None),
        P("ctx", None),
        P("ctx"),
        P("ctx", None),
        P("dp", None),
    )
    return jax.shard_map(
        local, mesh=mesh, in_specs=placed, out_specs=P("dp", "ctx", None), check_vma=False
    )
```

```python
import functools
import math

import jax
import jax.numpy as jnp
from jax import lax
from jax.experimental import pallas as pl
from jax.experimental.pallas import tpu as pltpu
from jax.sharding import PartitionSpec as P

TILE = 64
REACH = 6
KMAX = 10
CAP = 2


def first_two(rows, rows_live, sources, tiles_per_device):
    local = jnp.arange(tiles_per_device, dtype=jnp.int32)
    wanted = sources[:, None] * tiles_per_device + local[None, :]
    named = jnp.any(
        (rows[:, :, :, None] == wanted[:, None, None, :]) & rows_live[:, :, :, None], axis=(1, 2)
    )
    order = jnp.where(named, local[None, :], tiles_per_device)
    first = jnp.min(order, axis=1)
    second = jnp.min(jnp.where(order > first[:, None], order, tiles_per_device), axis=1)
    first = jnp.where(first == tiles_per_device, 0, first)
    second = jnp.where(second == tiles_per_device, 0, second)
    return first.astype(jnp.int32), second.astype(jnp.int32)


def attention_kernel(pos_ref, count_ref, bias_ref, q_ref, own_ref, far_ref, out_ref, *, heads, head_size, scale):
    tile = pl.program_id(0)
    own_tiles = own_ref.shape[0]
    live_count = count_ref[tile]
    queries = q_ref[0]
    picks = []
    for slot in range(KMAX):
        where = pos_ref[tile, slot]
        picks.append((
            where < own_tiles,
            jnp.minimum(where, own_tiles - 1),
            jnp.maximum(where - own_tiles, 0),
        ))

    def rows(part, slot, cols):
        mine, near, far = picks[slot]
        return jnp.where(mine, own_ref[near, part, 0, :, cols], far_ref[far, part, 0, :, cols])

    column = lax.broadcasted_iota(jnp.int32, (1, KMAX * TILE), 1) // TILE
    live = column < live_count
    for head in range(heads):
        cols = pl.ds(head * head_size, head_size)
        q_head = queries[:, head * head_size:(head + 1) * head_size]
        keys = jnp.concatenate([rows(0, slot, cols) for slot in range(KMAX)], axis=0)
        values = jnp.concatenate([rows(1, slot, cols) for slot in range(KMAX)], axis=0)
        bias_row = jnp.zeros((1, KMAX * TILE), jnp.float32)
        for slot in range(KMAX):
            bias_row = jnp.where(column == slot, bias_ref[tile, head, slot], bias_row)
        s = lax.dot_general(
            q_head, keys, (((1,), (1,)), ((), ())), preferred_element_type=jnp.float32
        )
        s = jnp.where(live, s * scale + bias_row, -1e30)
        row_max = s.max(axis=1, keepdims=True)
        w = jnp.exp(s - row_max)
        weight_sum = w.sum(axis=1, keepdims=True)
        total = jnp.dot(w.astype(jnp.bfloat16), values, preferred_element_type=jnp.float32)
        out_ref[0, :, head * head_size:(head + 1) * head_size] = (total / weight_sum).astype(out_ref.dtype)


def attend(positions, live_counts, bias, queries, own_tiles, far_tiles, heads, head_size):
    _, token_count, width = queries.shape
    tile_count = token_count // TILE

    def whole(array):
        return pl.BlockSpec(array.shape, lambda t, pos, cnt: (0,) * array.ndim)

    kernel = functools.partial(
        attention_kernel, heads=heads, head_size=head_size, scale=1.0 / math.sqrt(head_size)
    )
    return pl.pallas_call(
        kernel,
        out_shape=jax.ShapeDtypeStruct((1, token_count, width), jnp.bfloat16),
        grid_spec=pltpu.PrefetchScalarGridSpec(
            num_scalar_prefetch=2,
            grid=(tile_count,),
            in_specs=[pl.BlockSpec(memory_space=pltpu.SMEM),
                      pl.BlockSpec((1, TILE, width), lambda t, pos, cnt: (0, t, 0)),
                      whole(own_tiles), whole(far_tiles)],
            out_specs=pl.BlockSpec((1, TILE, width), lambda t, pos, cnt: (0, t, 0)),
        ),
    )(positions, live_counts, bias, queries, own_tiles, far_tiles)


def partner_pairs(count, step):
    return [(source, source ^ step) for source in range(count)]


def local(clip_tokens, qkv_weight, out_weight, neighbours, counts, bias_index, rel_bias):
    heads_here = rel_bias.shape[0]
    width_here = out_weight.shape[0]
    head_size = width_here // heads_here
    token_count = clip_tokens.shape[1]
    tile_count = token_count // TILE
    n_ctx = lax.axis_size("ctx")
    n_dp = lax.axis_size("dp")
    own_index = lax.axis_index("ctx").astype(jnp.int32)
    devices = jnp.arange(n_ctx, dtype=jnp.int32)

    table = jnp.concatenate([neighbours, counts[:, None]], axis=1).astype(jnp.float32)
    all_table = lax.all_gather(table, "ctx", axis=0, tiled=True).astype(jnp.int32)
    all_table = all_table.reshape(n_ctx, tile_count, KMAX + 1)
    all_live = jnp.arange(KMAX)[None, None, :] < all_table[:, :, KMAX:]
    send_first, send_second = first_two(
        all_table[:, :, :KMAX], all_live, jnp.full((n_ctx,), own_index), tile_count
    )
    send_picks = jnp.stack([send_first, send_second], axis=1).reshape(-1)

    live = jnp.arange(KMAX)[None, :] < counts[:, None]
    recv_first, _ = first_two(
        jnp.broadcast_to(neighbours[None], (n_ctx,) + neighbours.shape),
        jnp.broadcast_to(live[None], (n_ctx,) + live.shape),
        devices,
        tile_count,
    )
    source = neighbours // tile_count
    within = neighbours % tile_count
    remote_slot = tile_count + CAP * source + jnp.where(within == recv_first[source], 0, 1)
    positions = jnp.where(source == own_index, within, remote_slot).astype(jnp.int32)
    bias = jnp.transpose(jnp.take(rel_bias, bias_index, axis=1), (1, 0, 2))
    live_counts = counts.astype(jnp.int32)

    own_tokens = clip_tokens[0]
    order = [3, 1, 2, 0] if n_dp == 4 else list(range(1, n_dp)) + [0]
    arrived = {0: own_tokens}
    for step in range(1, n_dp):
        arrived[step] = lax.ppermute(own_tokens, "dp", partner_pairs(n_dp, step))
    total = None
    received = []
    partials = []
    sent = []
    for index, step in enumerate(order):
        tokens = arrived[step]
        if index >= 2:
            tokens, _ = lax.optimization_barrier((tokens, received[index - 2]))
        key_value = jnp.einsum(
            "td,sdh->sth", tokens, qkv_weight[1:3], preferred_element_type=jnp.float32
        ).astype(jnp.bfloat16)
        by_tile = jnp.transpose(
            key_value.reshape(2, tile_count, TILE, width_here), (1, 0, 2, 3)
        )[:, :, None]
        payload = by_tile.at[send_picks].get(mode="promise_in_bounds")
        if index >= 2:
            payload, _ = lax.optimization_barrier((payload, partials[index - 2]))
        if index == len(order) - 1 and len(sent) >= 2:
            payload, _ = lax.optimization_barrier((payload, sent[-3]))
        incoming = lax.all_to_all(payload, "ctx", 0, 0, tiled=True)
        received.append(incoming)
        if index == len(order) - 1 and len(sent) >= 2:
            incoming, _ = lax.optimization_barrier((incoming, sent[-2]))
        queries = jnp.dot(tokens, qkv_weight[0], preferred_element_type=jnp.float32).astype(jnp.bfloat16)
        attended = attend(positions, live_counts, bias, queries[None], by_tile, incoming, heads_here, head_size)
        partial_out = jnp.dot(
            attended[0], out_weight, preferred_element_type=jnp.float32
        ).astype(jnp.bfloat16)
        partials.append(partial_out)
        if step > 0:
            partial_out = lax.ppermute(partial_out, "dp", partner_pairs(n_dp, step))
            sent.append(partial_out)
        contribution = partial_out.astype(jnp.float32)
        total = contribution if total is None else total + contribution
    return total.astype(jnp.bfloat16)[None]


def solution(mesh):
    placed = (
        P("dp", "ctx", None),
        P(None, None, "dp"),
        P("dp", None),
        P("ctx", None),
        P("ctx"),
        P("ctx", None),
        P("dp", None),
    )
    return jax.shard_map(
        local, mesh=mesh, in_specs=placed, out_specs=P("dp", "ctx", None), check_vma=False
    )
```

```python
import functools
import math

import jax
import jax.numpy as jnp
from jax import lax
from jax.experimental import pallas as pl
from jax.experimental.pallas import tpu as pltpu
from jax.sharding import PartitionSpec as P

TILE = 64
REACH = 6
KMAX = 10
CAP = 2


def first_two(rows, rows_live, sources, tiles_per_device):
    local = jnp.arange(tiles_per_device, dtype=jnp.int32)
    wanted = sources[:, None] * tiles_per_device + local[None, :]
    named = jnp.any(
        (rows[:, :, :, None] == wanted[:, None, None, :]) & rows_live[:, :, :, None], axis=(1, 2)
    )
    order = jnp.where(named, local[None, :], tiles_per_device)
    first = jnp.min(order, axis=1)
    second = jnp.min(jnp.where(order > first[:, None], order, tiles_per_device), axis=1)
    first = jnp.where(first == tiles_per_device, 0, first)
    second = jnp.where(second == tiles_per_device, 0, second)
    return first.astype(jnp.int32), second.astype(jnp.int32)


def attention_kernel(pos_ref, count_ref, bias_ref, q_ref, own_ref, far_ref, out_ref, pool_ref, *, heads, head_size, scale):
    tile = pl.program_id(0)
    own_tiles = own_ref.shape[0]
    live_count = count_ref[tile]
    queries = q_ref[0]

    @pl.when(tile == 0)
    def _():
        pool_ref[:own_tiles] = own_ref[...]
        pool_ref[own_tiles:] = far_ref[...]

    def rows(part, slot, cols):
        return pool_ref[pos_ref[tile, slot], part, 0, :, cols]

    column = lax.broadcasted_iota(jnp.int32, (1, KMAX * TILE), 1) // TILE
    live = column < live_count
    for head in range(heads):
        cols = pl.ds(head * head_size, head_size)
        q_head = queries[:, head * head_size:(head + 1) * head_size]
        keys = jnp.concatenate([rows(0, slot, cols) for slot in range(KMAX)], axis=0)
        values = jnp.concatenate([rows(1, slot, cols) for slot in range(KMAX)], axis=0)
        bias_row = jnp.zeros((1, KMAX * TILE), jnp.float32)
        for slot in range(KMAX):
            bias_row = jnp.where(column == slot, bias_ref[tile, head, slot], bias_row)
        s = lax.dot_general(
            q_head, keys, (((1,), (1,)), ((), ())), preferred_element_type=jnp.float32
        )
        s = jnp.where(live, s * scale + bias_row, -1e30)
        row_max = s.max(axis=1, keepdims=True)
        w = jnp.exp(s - row_max)
        weight_sum = w.sum(axis=1, keepdims=True)
        total = jnp.dot(w.astype(jnp.bfloat16), values, preferred_element_type=jnp.float32)
        out_ref[0, :, head * head_size:(head + 1) * head_size] = (total / weight_sum).astype(out_ref.dtype)


def attend(positions, live_counts, bias, queries, own_tiles, far_tiles, heads, head_size):
    _, token_count, width = queries.shape
    tile_count = token_count // TILE

    def whole(array):
        return pl.BlockSpec(array.shape, lambda t, pos, cnt: (0,) * array.ndim)

    kernel = functools.partial(
        attention_kernel, heads=heads, head_size=head_size, scale=1.0 / math.sqrt(head_size)
    )
    return pl.pallas_call(
        kernel,
        out_shape=jax.ShapeDtypeStruct((1, token_count, width), jnp.bfloat16),
        grid_spec=pltpu.PrefetchScalarGridSpec(
            num_scalar_prefetch=2,
            grid=(tile_count,),
            in_specs=[pl.BlockSpec(memory_space=pltpu.SMEM),
                      pl.BlockSpec((1, TILE, width), lambda t, pos, cnt: (0, t, 0)),
                      whole(own_tiles), whole(far_tiles)],
            out_specs=pl.BlockSpec((1, TILE, width), lambda t, pos, cnt: (0, t, 0)),
            scratch_shapes=[pltpu.VMEM(
                (own_tiles.shape[0] + far_tiles.shape[0],) + own_tiles.shape[1:], own_tiles.dtype
            )],
        ),
    )(positions, live_counts, bias, queries, own_tiles, far_tiles)


def partner_pairs(count, step):
    return [(source, source ^ step) for source in range(count)]


def local(clip_tokens, qkv_weight, out_weight, neighbours, counts, bias_index, rel_bias):
    heads_here = rel_bias.shape[0]
    width_here = out_weight.shape[0]
    head_size = width_here // heads_here
    token_count = clip_tokens.shape[1]
    tile_count = token_count // TILE
    n_ctx = lax.axis_size("ctx")
    n_dp = lax.axis_size("dp")
    own_index = lax.axis_index("ctx").astype(jnp.int32)
    devices = jnp.arange(n_ctx, dtype=jnp.int32)

    table = jnp.concatenate([neighbours, counts[:, None]], axis=1).astype(jnp.float32)
    all_table = lax.all_gather(table, "ctx", axis=0, tiled=True).astype(jnp.int32)
    all_table = all_table.reshape(n_ctx, tile_count, KMAX + 1)
    all_live = jnp.arange(KMAX)[None, None, :] < all_table[:, :, KMAX:]
    send_first, send_second = first_two(
        all_table[:, :, :KMAX], all_live, jnp.full((n_ctx,), own_index), tile_count
    )
    send_picks = jnp.stack([send_first, send_second], axis=1).reshape(-1)

    live = jnp.arange(KMAX)[None, :] < counts[:, None]
    recv_first, _ = first_two(
        jnp.broadcast_to(neighbours[None], (n_ctx,) + neighbours.shape),
        jnp.broadcast_to(live[None], (n_ctx,) + live.shape),
        devices,
        tile_count,
    )
    source = neighbours // tile_count
    within = neighbours % tile_count
    remote_slot = tile_count + CAP * source + jnp.where(within == recv_first[source], 0, 1)
    positions = jnp.where(source == own_index, within, remote_slot).astype(jnp.int32)
    bias = jnp.transpose(jnp.take(rel_bias, bias_index, axis=1), (1, 0, 2))
    live_counts = counts.astype(jnp.int32)

    own_tokens = clip_tokens[0]
    order = [3, 1, 2, 0] if n_dp == 4 else list(range(1, n_dp)) + [0]
    arrived = {0: own_tokens}
    for step in range(1, n_dp):
        arrived[step] = lax.ppermute(own_tokens, "dp", partner_pairs(n_dp, step))
    total = None
    received = []
    partials = []
    sent = []
    for index, step in enumerate(order):
        tokens = arrived[step]
        if index >= 2:
            tokens, _ = lax.optimization_barrier((tokens, received[index - 2]))
        key_value = jnp.einsum(
            "td,sdh->sth", tokens, qkv_weight[1:3], preferred_element_type=jnp.float32
        ).astype(jnp.bfloat16)
        by_tile = jnp.transpose(
            key_value.reshape(2, tile_count, TILE, width_here), (1, 0, 2, 3)
        )[:, :, None]
        payload = by_tile.at[send_picks].get(mode="promise_in_bounds")
        if index >= 2:
            payload, _ = lax.optimization_barrier((payload, partials[index - 2]))
        if index == len(order) - 1 and len(sent) >= 2:
            payload, _ = lax.optimization_barrier((payload, sent[-3]))
        incoming = lax.all_to_all(payload, "ctx", 0, 0, tiled=True)
        received.append(incoming)
        if index == len(order) - 1 and len(sent) >= 2:
            incoming, _ = lax.optimization_barrier((incoming, sent[-2]))
        queries = jnp.dot(tokens, qkv_weight[0], preferred_element_type=jnp.float32).astype(jnp.bfloat16)
        attended = attend(positions, live_counts, bias, queries[None], by_tile, incoming, heads_here, head_size)
        partial_out = jnp.dot(
            attended[0], out_weight, preferred_element_type=jnp.float32
        ).astype(jnp.bfloat16)
        partials.append(partial_out)
        if step > 0:
            partial_out = lax.ppermute(partial_out, "dp", partner_pairs(n_dp, step))
            sent.append(partial_out)
        contribution = partial_out.astype(jnp.float32)
        total = contribution if total is None else total + contribution
    return total.astype(jnp.bfloat16)[None]


def solution(mesh):
    placed = (
        P("dp", "ctx", None),
        P(None, None, "dp"),
        P("dp", None),
        P("ctx", None),
        P("ctx"),
        P("ctx", None),
        P("dp", None),
    )
    return jax.shard_map(
        local, mesh=mesh, in_specs=placed, out_specs=P("dp", "ctx", None), check_vma=False
    )
```

```python
import functools
import math

import jax
import jax.numpy as jnp
from jax import lax
from jax.experimental import pallas as pl
from jax.experimental.pallas import tpu as pltpu
from jax.sharding import PartitionSpec as P

TILE = 64
REACH = 6
KMAX = 10
CAP = 2


def first_two(rows, rows_live, sources, tiles_per_device):
    local = jnp.arange(tiles_per_device, dtype=jnp.int32)
    wanted = sources[:, None] * tiles_per_device + local[None, :]
    named = jnp.any(
        (rows[:, :, :, None] == wanted[:, None, None, :]) & rows_live[:, :, :, None], axis=(1, 2)
    )
    order = jnp.where(named, local[None, :], tiles_per_device)
    first = jnp.min(order, axis=1)
    second = jnp.min(jnp.where(order > first[:, None], order, tiles_per_device), axis=1)
    first = jnp.where(first == tiles_per_device, 0, first)
    second = jnp.where(second == tiles_per_device, 0, second)
    return first.astype(jnp.int32), second.astype(jnp.int32)


def attention_kernel(pos_ref, count_ref, bias_ref, q_ref, own_ref, far_ref, out_ref, *, heads, head_size, scale, first):
    tile = pl.program_id(0) + first
    own_tiles = own_ref.shape[0]
    live_count = count_ref[tile]
    queries = q_ref[0]
    picks = []
    for slot in range(KMAX):
        where = pos_ref[tile, slot]
        picks.append((
            where < own_tiles,
            jnp.minimum(where, own_tiles - 1),
            jnp.maximum(where - own_tiles, 0),
        ))

    def rows(part, slot, cols):
        mine, near, far = picks[slot]
        return jnp.where(mine, own_ref[near, part, 0, :, cols], far_ref[far, part, 0, :, cols])

    column = lax.broadcasted_iota(jnp.int32, (1, KMAX * TILE), 1) // TILE
    live = column < live_count
    for head in range(heads):
        cols = pl.ds(head * head_size, head_size)
        q_head = queries[:, head * head_size:(head + 1) * head_size]
        keys = jnp.concatenate([rows(0, slot, cols) for slot in range(KMAX)], axis=0)
        values = jnp.concatenate([rows(1, slot, cols) for slot in range(KMAX)], axis=0)
        bias_row = jnp.zeros((1, KMAX * TILE), jnp.float32)
        for slot in range(KMAX):
            bias_row = jnp.where(column == slot, bias_ref[tile, head, slot], bias_row)
        s = lax.dot_general(
            q_head, keys, (((1,), (1,)), ((), ())), preferred_element_type=jnp.float32
        )
        s = jnp.where(live, s * scale + bias_row, -1e30)
        row_max = s.max(axis=1, keepdims=True)
        w = jnp.exp(s - row_max)
        weight_sum = w.sum(axis=1, keepdims=True)
        total = jnp.dot(w.astype(jnp.bfloat16), values, preferred_element_type=jnp.float32)
        out_ref[0, :, head * head_size:(head + 1) * head_size] = (total / weight_sum).astype(out_ref.dtype)


def attend(positions, live_counts, bias, queries, own_tiles, far_tiles, heads, head_size, first=0, count=None):
    _, token_count, width = queries.shape
    tile_count = token_count // TILE if count is None else count

    def whole(array):
        return pl.BlockSpec(array.shape, lambda t, pos, cnt: (0,) * array.ndim)

    kernel = functools.partial(
        attention_kernel, heads=heads, head_size=head_size, scale=1.0 / math.sqrt(head_size), first=first
    )
    return pl.pallas_call(
        kernel,
        out_shape=jax.ShapeDtypeStruct((1, tile_count * TILE, width), jnp.bfloat16),
        grid_spec=pltpu.PrefetchScalarGridSpec(
            num_scalar_prefetch=2,
            grid=(tile_count,),
            in_specs=[pl.BlockSpec(memory_space=pltpu.SMEM),
                      pl.BlockSpec((1, TILE, width), lambda t, pos, cnt: (0, t + first, 0)),
                      whole(own_tiles), whole(far_tiles)],
            out_specs=pl.BlockSpec((1, TILE, width), lambda t, pos, cnt: (0, t, 0)),
        ),
    )(positions, live_counts, bias, queries, own_tiles, far_tiles)


def partner_pairs(count, step):
    return [(source, source ^ step) for source in range(count)]


def local(clip_tokens, qkv_weight, out_weight, neighbours, counts, bias_index, rel_bias):
    heads_here = rel_bias.shape[0]
    width_here = out_weight.shape[0]
    head_size = width_here // heads_here
    token_count = clip_tokens.shape[1]
    tile_count = token_count // TILE
    n_ctx = lax.axis_size("ctx")
    n_dp = lax.axis_size("dp")
    own_index = lax.axis_index("ctx").astype(jnp.int32)
    devices = jnp.arange(n_ctx, dtype=jnp.int32)

    table = jnp.concatenate([neighbours, counts[:, None]], axis=1).astype(jnp.float32)
    all_table = lax.all_gather(table, "ctx", axis=0, tiled=True).astype(jnp.int32)
    all_table = all_table.reshape(n_ctx, tile_count, KMAX + 1)
    all_live = jnp.arange(KMAX)[None, None, :] < all_table[:, :, KMAX:]
    send_first, send_second = first_two(
        all_table[:, :, :KMAX], all_live, jnp.full((n_ctx,), own_index), tile_count
    )
    send_picks = jnp.stack([send_first, send_second], axis=1).reshape(-1)

    live = jnp.arange(KMAX)[None, :] < counts[:, None]
    recv_first, _ = first_two(
        jnp.broadcast_to(neighbours[None], (n_ctx,) + neighbours.shape),
        jnp.broadcast_to(live[None], (n_ctx,) + live.shape),
        devices,
        tile_count,
    )
    source = neighbours // tile_count
    within = neighbours % tile_count
    remote_slot = tile_count + CAP * source + jnp.where(within == recv_first[source], 0, 1)
    positions = jnp.where(source == own_index, within, remote_slot).astype(jnp.int32)
    bias = jnp.transpose(jnp.take(rel_bias, bias_index, axis=1), (1, 0, 2))
    live_counts = counts.astype(jnp.int32)

    own_tokens = clip_tokens[0]
    order = [3, 1, 2, 0] if n_dp == 4 else list(range(1, n_dp)) + [0]
    arrived = {0: own_tokens}
    for step in range(1, n_dp):
        arrived[step] = lax.ppermute(own_tokens, "dp", partner_pairs(n_dp, step))
    total = None
    received = []
    partials = []
    sent = []
    for index, step in enumerate(order):
        tokens = arrived[step]
        if index >= 2:
            tokens, _ = lax.optimization_barrier((tokens, received[index - 2]))
        key_value = jnp.einsum(
            "td,sdh->sth", tokens, qkv_weight[1:3], preferred_element_type=jnp.float32
        ).astype(jnp.bfloat16)
        by_tile = jnp.transpose(
            key_value.reshape(2, tile_count, TILE, width_here), (1, 0, 2, 3)
        )[:, :, None]
        payload = by_tile.at[send_picks].get(mode="promise_in_bounds")
        if index >= 2:
            payload, _ = lax.optimization_barrier((payload, partials[index - 2]))
        if index == len(order) - 1 and len(sent) >= 2:
            payload, _ = lax.optimization_barrier((payload, sent[-3]))
        incoming = lax.all_to_all(payload, "ctx", 0, 0, tiled=True)
        received.append(incoming)
        if index == len(order) - 1 and len(sent) >= 2:
            incoming, _ = lax.optimization_barrier((incoming, sent[-2]))
        queries = jnp.dot(tokens, qkv_weight[0], preferred_element_type=jnp.float32).astype(jnp.bfloat16)
        if index == len(order) - 2 and step > 0 and tile_count % 2 == 0:
            halves = []
            for first in (0, tile_count // 2):
                part = attend(
                    positions, live_counts, bias, queries[None], by_tile, incoming, heads_here, head_size,
                    first, tile_count // 2,
                )
                part = jnp.dot(part[0], out_weight, preferred_element_type=jnp.float32).astype(jnp.bfloat16)
                halves.append(lax.ppermute(part, "dp", partner_pairs(n_dp, step)))
            partial_out = jnp.concatenate(halves, axis=0)
            partials.append(partial_out)
            sent.append(partial_out)
        else:
            attended = attend(
                positions, live_counts, bias, queries[None], by_tile, incoming, heads_here, head_size
            )
            partial_out = jnp.dot(
                attended[0], out_weight, preferred_element_type=jnp.float32
            ).astype(jnp.bfloat16)
            partials.append(partial_out)
            if step > 0:
                partial_out = lax.ppermute(partial_out, "dp", partner_pairs(n_dp, step))
                sent.append(partial_out)
        contribution = partial_out.astype(jnp.float32)
        total = contribution if total is None else total + contribution
    return total.astype(jnp.bfloat16)[None]


def solution(mesh):
    placed = (
        P("dp", "ctx", None),
        P(None, None, "dp"),
        P("dp", None),
        P("ctx", None),
        P("ctx"),
        P("ctx", None),
        P("dp", None),
    )
    return jax.shard_map(
        local, mesh=mesh, in_specs=placed, out_specs=P("dp", "ctx", None), check_vma=False
    )
```

```python
import functools
import math

import jax
import jax.numpy as jnp
from jax import lax
from jax.experimental import pallas as pl
from jax.experimental.pallas import tpu as pltpu
from jax.sharding import PartitionSpec as P

TILE = 64
REACH = 6
KMAX = 10
CAP = 2


def first_two(rows, rows_live, sources, tiles_per_device):
    local = jnp.arange(tiles_per_device, dtype=jnp.int32)
    wanted = sources[:, None] * tiles_per_device + local[None, :]
    named = jnp.any(
        (rows[:, :, :, None] == wanted[:, None, None, :]) & rows_live[:, :, :, None], axis=(1, 2)
    )
    order = jnp.where(named, local[None, :], tiles_per_device)
    first = jnp.min(order, axis=1)
    second = jnp.min(jnp.where(order > first[:, None], order, tiles_per_device), axis=1)
    first = jnp.where(first == tiles_per_device, 0, first)
    second = jnp.where(second == tiles_per_device, 0, second)
    return first.astype(jnp.int32), second.astype(jnp.int32)


def attention_kernel(pos_ref, count_ref, bias_ref, q_ref, own_ref, far_ref, out_ref, *, heads, head_size, scale):
    tile = pl.program_id(0)
    own_tiles = own_ref.shape[0]
    live_count = count_ref[tile]
    queries = q_ref[0]
    picks = []
    for slot in range(KMAX):
        where = pos_ref[tile, slot]
        picks.append((
            where < own_tiles,
            jnp.minimum(where, own_tiles - 1),
            jnp.maximum(where - own_tiles, 0),
        ))

    def rows(part, slot, cols):
        mine, near, far = picks[slot]
        return jnp.where(mine, own_ref[near, part, 0, :, cols], far_ref[far, part, 0, :, cols])

    column = lax.broadcasted_iota(jnp.int32, (1, KMAX * TILE), 1) // TILE
    live = column < live_count
    for head in range(heads):
        cols = pl.ds(head * head_size, head_size)
        q_head = queries[:, head * head_size:(head + 1) * head_size]
        keys = jnp.concatenate([rows(0, slot, cols) for slot in range(KMAX)], axis=0)
        values = jnp.concatenate([rows(1, slot, cols) for slot in range(KMAX)], axis=0)
        bias_row = jnp.zeros((1, KMAX * TILE), jnp.float32)
        for slot in range(KMAX):
            bias_row = jnp.where(column == slot, bias_ref[tile, head, slot], bias_row)
        s = lax.dot_general(
            q_head, keys, (((1,), (1,)), ((), ())), preferred_element_type=jnp.float32
        )
        s = jnp.where(live, s * scale + bias_row, -1e30)
        row_max = s.max(axis=1, keepdims=True)
        w = jnp.exp(s - row_max)
        weight_sum = w.sum(axis=1, keepdims=True)
        total = jnp.dot(w.astype(jnp.bfloat16), values, preferred_element_type=jnp.float32)
        out_ref[0, :, head * head_size:(head + 1) * head_size] = (total / weight_sum).astype(out_ref.dtype)


def attend(positions, live_counts, bias, queries, own_tiles, far_tiles, heads, head_size):
    _, token_count, width = queries.shape
    tile_count = token_count // TILE

    def whole(array):
        return pl.BlockSpec(array.shape, lambda t, pos, cnt: (0,) * array.ndim)

    kernel = functools.partial(
        attention_kernel, heads=heads, head_size=head_size, scale=1.0 / math.sqrt(head_size)
    )
    return pl.pallas_call(
        kernel,
        out_shape=jax.ShapeDtypeStruct((1, token_count, width), jnp.bfloat16),
        grid_spec=pltpu.PrefetchScalarGridSpec(
            num_scalar_prefetch=2,
            grid=(tile_count,),
            in_specs=[pl.BlockSpec(memory_space=pltpu.SMEM),
                      pl.BlockSpec((1, TILE, width), lambda t, pos, cnt: (0, t, 0)),
                      whole(own_tiles), whole(far_tiles)],
            out_specs=pl.BlockSpec((1, TILE, width), lambda t, pos, cnt: (0, t, 0)),
        ),
    )(positions, live_counts, bias, queries, own_tiles, far_tiles)


def partner_pairs(count, step):
    return [(source, source ^ step) for source in range(count)]


def local(clip_tokens, qkv_weight, out_weight, neighbours, counts, bias_index, rel_bias):
    heads_here = rel_bias.shape[0]
    width_here = out_weight.shape[0]
    head_size = width_here // heads_here
    token_count = clip_tokens.shape[1]
    tile_count = token_count // TILE
    n_ctx = lax.axis_size("ctx")
    n_dp = lax.axis_size("dp")
    own_index = lax.axis_index("ctx").astype(jnp.int32)
    devices = jnp.arange(n_ctx, dtype=jnp.int32)

    table = jnp.concatenate([neighbours, counts[:, None]], axis=1).astype(jnp.float32)
    all_table = lax.all_gather(table, "ctx", axis=0, tiled=True).astype(jnp.int32)
    all_table = all_table.reshape(n_ctx, tile_count, KMAX + 1)
    all_live = jnp.arange(KMAX)[None, None, :] < all_table[:, :, KMAX:]
    send_first, send_second = first_two(
        all_table[:, :, :KMAX], all_live, jnp.full((n_ctx,), own_index), tile_count
    )
    send_picks = jnp.stack([send_first, send_second], axis=1).reshape(-1)

    live = jnp.arange(KMAX)[None, :] < counts[:, None]
    recv_first, _ = first_two(
        jnp.broadcast_to(neighbours[None], (n_ctx,) + neighbours.shape),
        jnp.broadcast_to(live[None], (n_ctx,) + live.shape),
        devices,
        tile_count,
    )
    source = neighbours // tile_count
    within = neighbours % tile_count
    remote_slot = tile_count + CAP * source + jnp.where(within == recv_first[source], 0, 1)
    positions = jnp.where(source == own_index, within, remote_slot).astype(jnp.int32)
    bias = jnp.transpose(jnp.take(rel_bias, bias_index, axis=1), (1, 0, 2))
    live_counts = counts.astype(jnp.int32)

    own_tokens = clip_tokens[0]
    order = [3, 1, 2, 0] if n_dp == 4 else list(range(1, n_dp)) + [0]
    arrived = {0: own_tokens}
    for step in range(1, n_dp):
        arrived[step] = lax.ppermute(own_tokens, "dp", partner_pairs(n_dp, step))
    total = None
    received = []
    partials = []
    sent = []
    for index, step in enumerate(order):
        tokens = arrived[step]
        if index >= 2:
            tokens, _ = lax.optimization_barrier((tokens, received[index - 2]))
        projected = jnp.einsum(
            "td,sdh->sth", tokens, qkv_weight, preferred_element_type=jnp.float32
        ).astype(jnp.bfloat16)
        by_tile = jnp.transpose(
            projected[1:3].reshape(2, tile_count, TILE, width_here), (1, 0, 2, 3)
        )[:, :, None]
        payload = by_tile.at[send_picks].get(mode="promise_in_bounds")
        if index >= 2:
            payload, _ = lax.optimization_barrier((payload, partials[index - 2]))
        if index == len(order) - 1 and len(sent) >= 2:
            payload, _ = lax.optimization_barrier((payload, sent[-3]))
        incoming = lax.all_to_all(payload, "ctx", 0, 0, tiled=True)
        received.append(incoming)
        if index == len(order) - 1 and len(sent) >= 2:
            incoming, _ = lax.optimization_barrier((incoming, sent[-2]))
        attended = attend(positions, live_counts, bias, projected, by_tile, incoming, heads_here, head_size)
        partial_out = jnp.dot(
            attended[0], out_weight, preferred_element_type=jnp.float32
        ).astype(jnp.bfloat16)
        partials.append(partial_out)
        if step > 0:
            partial_out = lax.ppermute(partial_out, "dp", partner_pairs(n_dp, step))
            sent.append(partial_out)
        contribution = partial_out.astype(jnp.float32)
        if index == len(order) - 2 and len(order) > 1:
            late = contribution
            continue
        total = contribution if total is None else total + contribution
    if len(order) > 1:
        total = lax.optimization_barrier(total) + late
    return total.astype(jnp.bfloat16)[None]


def solution(mesh):
    placed = (
        P("dp", "ctx", None),
        P(None, None, "dp"),
        P("dp", None),
        P("ctx", None),
        P("ctx"),
        P("ctx", None),
        P("dp", None),
    )
    return jax.shard_map(
        local, mesh=mesh, in_specs=placed, out_specs=P("dp", "ctx", None), check_vma=False
    )
```

```python
import functools
import math

import jax
import jax.numpy as jnp
from jax import lax
from jax.experimental import pallas as pl
from jax.experimental.pallas import tpu as pltpu
from jax.sharding import PartitionSpec as P

TILE = 64
REACH = 6
KMAX = 10
CAP = 2


def first_two(rows, rows_live, sources, tiles_per_device):
    local = jnp.arange(tiles_per_device, dtype=jnp.int32)
    wanted = sources[:, None] * tiles_per_device + local[None, :]
    named = jnp.any(
        (rows[:, :, :, None] == wanted[:, None, None, :]) & rows_live[:, :, :, None], axis=(1, 2)
    )
    order = jnp.where(named, local[None, :], tiles_per_device)
    first = jnp.min(order, axis=1)
    second = jnp.min(jnp.where(order > first[:, None], order, tiles_per_device), axis=1)
    first = jnp.where(first == tiles_per_device, 0, first)
    second = jnp.where(second == tiles_per_device, 0, second)
    return first.astype(jnp.int32), second.astype(jnp.int32)


def attention_kernel(pos_ref, count_ref, bias_ref, q_ref, own_ref, far_ref, out_ref, *, heads, head_size, scale):
    tile = pl.program_id(0)
    own_tiles = own_ref.shape[0]
    live_count = count_ref[tile]
    queries = q_ref[0]
    picks = []
    for slot in range(KMAX):
        where = pos_ref[tile, slot]
        picks.append((
            where < own_tiles,
            jnp.minimum(where, own_tiles - 1),
            jnp.maximum(where - own_tiles, 0),
        ))

    def rows(part, slot, cols):
        mine, near, far = picks[slot]
        return jnp.where(mine, own_ref[near, part, 0, :, cols], far_ref[far, part, 0, :, cols])

    column = lax.broadcasted_iota(jnp.int32, (1, KMAX * TILE), 1) // TILE
    live = column < live_count
    for head in range(heads):
        cols = pl.ds(head * head_size, head_size)
        q_head = queries[:, head * head_size:(head + 1) * head_size]
        keys = jnp.concatenate([rows(0, slot, cols) for slot in range(KMAX)], axis=0)
        values = jnp.concatenate([rows(1, slot, cols) for slot in range(KMAX)], axis=0)
        bias_row = jnp.zeros((1, KMAX * TILE), jnp.float32)
        for slot in range(KMAX):
            bias_row = jnp.where(column == slot, bias_ref[tile, head, slot], bias_row)
        s = lax.dot_general(
            q_head, keys, (((1,), (1,)), ((), ())), preferred_element_type=jnp.float32
        )
        s = jnp.where(live, s * scale + bias_row, -1e30)
        row_max = s.max(axis=1, keepdims=True)
        w = jnp.exp(s - row_max)
        weight_sum = w.sum(axis=1, keepdims=True)
        total = jnp.dot(w.astype(jnp.bfloat16), values, preferred_element_type=jnp.float32)
        out_ref[0, :, head * head_size:(head + 1) * head_size] = (total / weight_sum).astype(out_ref.dtype)


def attend(positions, live_counts, bias, queries, own_tiles, far_tiles, heads, head_size):
    _, token_count, width = queries.shape
    tile_count = token_count // TILE

    def whole(array):
        return pl.BlockSpec(array.shape, lambda t, pos, cnt: (0,) * array.ndim)

    kernel = functools.partial(
        attention_kernel, heads=heads, head_size=head_size, scale=1.0 / math.sqrt(head_size)
    )
    return pl.pallas_call(
        kernel,
        out_shape=jax.ShapeDtypeStruct((1, token_count, width), jnp.bfloat16),
        grid_spec=pltpu.PrefetchScalarGridSpec(
            num_scalar_prefetch=2,
            grid=(tile_count,),
            in_specs=[pl.BlockSpec(memory_space=pltpu.SMEM),
                      pl.BlockSpec((1, TILE, width), lambda t, pos, cnt: (0, t, 0)),
                      whole(own_tiles), whole(far_tiles)],
            out_specs=pl.BlockSpec((1, TILE, width), lambda t, pos, cnt: (0, t, 0)),
        ),
    )(positions, live_counts, bias, queries, own_tiles, far_tiles)


def partner_pairs(count, step):
    return [(source, source ^ step) for source in range(count)]


def local(clip_tokens, qkv_weight, out_weight, neighbours, counts, bias_index, rel_bias):
    heads_here = rel_bias.shape[0]
    width_here = out_weight.shape[0]
    head_size = width_here // heads_here
    token_count = clip_tokens.shape[1]
    tile_count = token_count // TILE
    n_ctx = lax.axis_size("ctx")
    n_dp = lax.axis_size("dp")
    own_index = lax.axis_index("ctx").astype(jnp.int32)
    devices = jnp.arange(n_ctx, dtype=jnp.int32)

    table = jnp.concatenate([neighbours, counts[:, None]], axis=1).astype(jnp.float32)
    all_table = lax.all_gather(table, "ctx", axis=0, tiled=True).astype(jnp.int32)
    all_table = all_table.reshape(n_ctx, tile_count, KMAX + 1)
    all_live = jnp.arange(KMAX)[None, None, :] < all_table[:, :, KMAX:]
    send_first, send_second = first_two(
        all_table[:, :, :KMAX], all_live, jnp.full((n_ctx,), own_index), tile_count
    )
    send_picks = jnp.stack([send_first, send_second], axis=1).reshape(-1)

    live = jnp.arange(KMAX)[None, :] < counts[:, None]
    recv_first, _ = first_two(
        jnp.broadcast_to(neighbours[None], (n_ctx,) + neighbours.shape),
        jnp.broadcast_to(live[None], (n_ctx,) + live.shape),
        devices,
        tile_count,
    )
    source = neighbours // tile_count
    within = neighbours % tile_count
    remote_slot = tile_count + CAP * source + jnp.where(within == recv_first[source], 0, 1)
    positions = jnp.where(source == own_index, within, remote_slot).astype(jnp.int32)
    bias = jnp.transpose(jnp.take(rel_bias, bias_index, axis=1), (1, 0, 2))
    live_counts = counts.astype(jnp.int32)

    own_tokens = clip_tokens[0]
    order = [3, 1, 2, 0] if n_dp == 4 else list(range(1, n_dp)) + [0]
    arrived = {0: own_tokens}
    for step in range(1, n_dp):
        arrived[step] = lax.ppermute(own_tokens, "dp", partner_pairs(n_dp, step))
    total = None
    received = []
    partials = []
    sent = []
    for index, step in enumerate(order):
        tokens = arrived[step]
        if index >= 2:
            tokens, _ = lax.optimization_barrier((tokens, received[index - 2]))
        key_value = jnp.einsum(
            "td,sdh->sth", tokens, qkv_weight[1:3], preferred_element_type=jnp.float32
        ).astype(jnp.bfloat16)
        by_tile = jnp.transpose(
            key_value.reshape(2, tile_count, TILE, width_here), (1, 0, 2, 3)
        )[:, :, None]
        payload = by_tile.at[send_picks].get(mode="promise_in_bounds")
        if index >= 2:
            payload, _ = lax.optimization_barrier((payload, partials[index - 2]))
        if index == len(order) - 1 and len(sent) >= 2:
            payload, _ = lax.optimization_barrier((payload, sent[-3]))
        incoming = lax.all_to_all(payload, "ctx", 0, 0, tiled=True)
        received.append(incoming)
        if index == len(order) - 1 and len(sent) >= 2:
            incoming, _ = lax.optimization_barrier((incoming, sent[-2]))
        queries = jnp.dot(tokens, qkv_weight[0], preferred_element_type=jnp.float32).astype(jnp.bfloat16)
        attended = attend(positions, live_counts, bias, queries[None], by_tile, incoming, heads_here, head_size)
        partial_out = jnp.dot(
            attended[0], out_weight, preferred_element_type=jnp.float32
        ).astype(jnp.bfloat16)
        partials.append(partial_out)
        if step > 0:
            partial_out = lax.ppermute(partial_out, "dp", partner_pairs(n_dp, step))
            sent.append(partial_out)
        contribution = partial_out.astype(jnp.float32)
        if index == len(order) - 2 and len(order) > 1:
            late = contribution
            continue
        total = contribution if total is None else total + contribution
    if len(order) > 1:
        total = lax.optimization_barrier(total) + late
    return total.astype(jnp.bfloat16)[None]


def solution(mesh):
    placed = (
        P("dp", "ctx", None),
        P(None, None, "dp"),
        P("dp", None),
        P("ctx", None),
        P("ctx"),
        P("ctx", None),
        P("dp", None),
    )
    return jax.shard_map(
        local, mesh=mesh, in_specs=placed, out_specs=P("dp", "ctx", None), check_vma=False
    )
```
